512 devices in a mesh: region: 64 (over z, y), group: 8 (over x, core).
Axes of the slice: x: 4, y: 4, z: 16, core: 2. Of those that a mesh axis runs over, the one named last changes fastest.
Arguments:
- coefficients: float32 [512, 48, 2304], P(('region', 'group')), may hold values from -6 to 6
- box_offset: int32 [3, 512], P(None, ('region', 'group')), may hold values from 0 to 383, as said below
- occupation: float32 [512], P(('region', 'group')), may hold values from 0.5 to 2
- external_potential: bfloat16 [384, 36864], P('region'), may hold values from -3 to 3
- core_density: float32 [384, 36864], P('region'), may hold values from 0.1 to 0.5
Outputs:
- next_coefficients: float32 [512, 48, 2304], P(('region', 'group'))
- density: float32 [384, 36864], P('region')
The draws below stay inside these ranges and needn't reach their ends.
Inputs may be any that keep to these rules, and one draw needn't show every extreme that they name: For function f, held by region R = f // 8, box_offset[0, f] = (R 6 - 4 * 6 + e) mod 384 with 0 <= e <= 6; box_offset[1, f] and box_offset[2, f] are below 192.
All inputs are finite; a program needn't handle non-finite values.
Results may differ from the reference program's by a relative error of at most 0.00064.
Values may be sent and summed in bfloat16 or wider, within the bound.
No kernel may reach another device: no remote copies, remote signals or barrier semaphores. Data moves between devices by JAX's collectives and lax.ppermute only.
A program may use at most 64 MiB of HBM per device.

```python
import math
import jax
import jax.numpy as jnp
from jax import lax

BOX = 48
F_DEV = 1
SZ = 6
NXY = 192
STEPS = 2
NZ = 384
FUNCS = 512
REGION_FUNCS = 8
CELLS = 2304
GRID_CELLS = 36864
SPAN = 4


def draw_box_offset(key, part):
    plane_key = jax.random.fold_in(key, 101)
    row_key = jax.random.fold_in(key, 202)
    column_key = jax.random.fold_in(key, 303)
    holder = jnp.arange(FUNCS, dtype=jnp.int32) // REGION_FUNCS
    extra_planes = jax.random.randint(plane_key, (FUNCS,), 0, SZ + 1, dtype=jnp.int32)
    first_plane = jnp.mod(holder * SZ - SPAN * SZ + extra_planes, NZ)
    first_row = jax.random.randint(row_key, (FUNCS,), 0, NXY, dtype=jnp.int32)
    first_column = jax.random.randint(column_key, (FUNCS,), 0, NXY, dtype=jnp.int32)
    return jnp.stack([first_plane, first_row, first_column]).astype(jnp.int32)


def level_of(stream_key, shape, cuts, smallest, top_value):
    factor_of = 1.0
    for dim, shards_of in cuts:
        steps = jax.random.uniform(jax.random.fold_in(jax.random.fold_in(stream_key, 6), dim), (shards_of,), jnp.float32, smallest / len(cuts), top_value / len(cuts))
        factor_of = factor_of * jnp.repeat(jnp.exp(steps), shape[dim] // shards_of).reshape((-1,) + (1,) * (len(shape) - 1 - dim))
    return factor_of


def normal_values(key, shape, scale, bound, cuts=(), kind=jnp.bfloat16):
    result = jax.random.normal(key, shape, jnp.float32) * scale
    if len(cuts) > 0:
        result = level_of(key, shape, cuts, -0.22, 0.18) * result
    return jnp.clip(result, min=-bound, max=bound).astype(kind)


def setup_inputs(seed: int = 0) -> dict:
    keys = jax.random.split(jax.random.key(seed), 6)
    coefficients = normal_values(keys[0], (FUNCS, BOX, CELLS), 1.0, 6.0, ((0, 512),), jnp.float32)
    box_offset = draw_box_offset(jax.random.fold_in(keys[5], 71), 0)
    occupation = jnp.clip(jnp.exp(math.log(2.0) - 1.3862944 * jax.random.uniform(keys[2], (FUNCS,), jnp.float32) ** level_of(keys[2], (FUNCS,), ((0, 512),), -0.2, 0.2)), 0.5, 2.0)
    external_potential = normal_values(keys[3], (NZ, GRID_CELLS), 0.5, 3.0, ((0, 64),))
    core_density = jnp.clip(0.1 + 0.4 * jax.random.uniform(keys[4], (NZ, GRID_CELLS), jnp.float32) ** level_of(keys[4], (NZ, GRID_CELLS), ((0, 64),), -0.2, 0.2), 0.1, 0.5)
    return dict(coefficients=coefficients, box_offset=box_offset, occupation=occupation, external_potential=external_potential, core_density=core_density)


step_size = 0.1
highest = lax.Precision.HIGHEST

def filter_matrix(extent):
    offset_index = (jnp.arange(extent)[:, None] - jnp.arange(extent)[None, :] + 8).astype(jnp.float32)
    tap_grid = jnp.arange(16).astype(jnp.float32)
    tap_values = jnp.exp(-0.5 * ((tap_grid - 7.5) / 1.2) ** 2)
    norm_value = jnp.sqrt(jnp.sum(tap_values * tap_values))
    values = jnp.exp(-0.5 * ((offset_index - 7.5) / 1.2) ** 2) / norm_value
    inside = (offset_index >= 0.0) & (offset_index <= 15.0)
    return jnp.where(inside, values, 0.0).astype(jnp.float32)

def kinetic_matrix(extent):
    distance = jnp.arange(extent)[:, None] - jnp.arange(extent)[None, :]
    magnitude = jnp.abs(distance)
    parity = 1.0 - 2.0 * (magnitude % 2).astype(jnp.float32)
    spread = jnp.maximum(magnitude, 1).astype(jnp.float32)
    values = parity / (spread * spread)
    values = jnp.where(magnitude == 0, math.pi ** 2 / 6.0, values)
    return jnp.where(magnitude <= 14, values, 0.0).astype(jnp.float32)

def separable(matrix, box_values):
    members, extent, plane_cells = box_values.shape
    cube_values = box_values.reshape(members, extent, extent, extent)
    cube_values = jnp.einsum('ij,fjyx->fiyx', matrix, cube_values, precision=highest)
    cube_values = jnp.einsum('ij,fzjx->fzix', matrix, cube_values, precision=highest)
    cube_values = jnp.einsum('ij,fzyj->fzyi', matrix, cube_values, precision=highest)
    return cube_values.reshape(members, extent, plane_cells)

def kinetic_term(matrix, box_values):
    members, extent, plane_cells = box_values.shape
    cube_values = box_values.reshape(members, extent, extent, extent)
    along_planes = jnp.einsum('ij,fjyx->fiyx', matrix, cube_values, precision=highest)
    along_rows = jnp.einsum('ij,fzjx->fzix', matrix, cube_values, precision=highest)
    along_columns = jnp.einsum('ij,fzyj->fzyi', matrix, cube_values, precision=highest)
    return (along_planes + along_rows + along_columns).reshape(members, extent, plane_cells)

def potential_of(external, rho_values):
    return (external.astype(jnp.float32) - jnp.cbrt(3.0 / math.pi * rho_values)).astype(jnp.bfloat16)

def fold_axis(values, dimension, extent, length):
    head_part = lax.slice_in_dim(values, 0, length, axis=dimension)
    tail_part = lax.slice_in_dim(values, length, length + extent, axis=dimension)
    widths = [(0, length - extent) if position == dimension else (0, 0) for position in range(values.ndim)]
    return head_part + jnp.pad(tail_part, widths)

def extend_axis(values, dimension, extent):
    return jnp.concatenate([values, lax.slice_in_dim(values, 0, extent, axis=dimension)], axis=dimension)

def reference(coefficients, box_offset, occupation, external_potential, core_density):
    synthesis = filter_matrix(BOX)
    kinetic_op = kinetic_matrix(BOX)
    coverage = float(NZ * GRID_CELLS) / float(FUNCS * BOX ** 3)
    blocks = FUNCS // F_DEV
    corners = jnp.transpose(box_offset.reshape(3, blocks, F_DEV), (1, 0, 2))
    weight_blocks = (coverage * occupation).reshape(blocks, F_DEV)
    current = coefficients.reshape(blocks, F_DEV, BOX, CELLS)
    rho_values = None
    for sweep_index in range(STEPS):

        def add_block(grid_pad, block_data):
            box_values, block_corners, block_weights = block_data
            orbital = separable(synthesis, box_values)
            weighted = (block_weights[:, None, None] * orbital * orbital).reshape(F_DEV, BOX, BOX, BOX)
            for member in range(F_DEV):
                corner = (block_corners[0, member], block_corners[1, member], block_corners[2, member])
                present = lax.dynamic_slice(grid_pad, corner, (BOX, BOX, BOX))
                grid_pad = lax.dynamic_update_slice(grid_pad, present + weighted[member], corner)
            return (grid_pad, None)
        empty_grid = jnp.zeros((NZ + BOX, NXY + BOX, NXY + BOX), jnp.float32)
        grid_pad, unused = lax.scan(add_block, empty_grid, (current, corners, weight_blocks))
        grid_sum = fold_axis(fold_axis(fold_axis(grid_pad, 0, BOX, NZ), 1, BOX, NXY), 2, BOX, NXY)
        rho_values = grid_sum.reshape(NZ, GRID_CELLS) + core_density
        potential = potential_of(external_potential, rho_values).reshape(NZ, NXY, NXY)
        potential_pad = extend_axis(extend_axis(extend_axis(potential, 0, BOX), 1, BOX), 2, BOX)

        def update(block_data):
            box_values, block_corners = block_data
            orbital = separable(synthesis, box_values)
            windows = jnp.stack([lax.dynamic_slice(potential_pad, (block_corners[0, member], block_corners[1, member], block_corners[2, member]), (BOX, BOX, BOX)).reshape(BOX, CELLS) for member in range(F_DEV)]).astype(jnp.float32)
            gradient = kinetic_term(kinetic_op, box_values) + separable(synthesis.T, windows * orbital)
            return box_values - step_size * gradient
        current = lax.map(update, (current, corners))
    return (current.reshape(FUNCS, BOX, CELLS), rho_values)
```

```python
import math

import jax
import jax.numpy as jnp
from jax import lax
from jax.sharding import PartitionSpec as P

STEPS = 2

step_size = 0.1
highest = lax.Precision.HIGHEST


def passed_along(value, axis, by):
    count = lax.axis_size(axis)
    return lax.ppermute(value, axis, [(i, (i + by) % count) for i in range(count)])


def filter_matrix(extent):
    offset_index = (jnp.arange(extent)[:, None] - jnp.arange(extent)[None, :] + 8).astype(
        jnp.float32
    )
    tap_grid = jnp.arange(16).astype(jnp.float32)
    tap_values = jnp.exp(-0.5 * ((tap_grid - 7.5) / 1.2) ** 2)
    norm_value = jnp.sqrt(jnp.sum(tap_values * tap_values))
    values = jnp.exp(-0.5 * ((offset_index - 7.5) / 1.2) ** 2) / norm_value
    inside = (offset_index >= 0.0) & (offset_index <= 15.0)
    return jnp.where(inside, values, 0.0)


def kinetic_matrix(extent):
    distance = jnp.arange(extent)[:, None] - jnp.arange(extent)[None, :]
    magnitude = jnp.abs(distance)
    parity = 1.0 - 2.0 * (magnitude % 2).astype(jnp.float32)
    spread = jnp.maximum(magnitude, 1).astype(jnp.float32)
    values = parity / (spread * spread)
    values = jnp.where(magnitude == 0, math.pi**2 / 6.0, values)
    return jnp.where(magnitude <= 14, values, 0.0)


def separable(matrix, box_values):
    members, extent, plane_cells = box_values.shape
    cube_values = box_values.reshape(members, extent, extent, extent)
    cube_values = jnp.einsum("ij,fjyx->fiyx", matrix, cube_values, precision=highest)
    cube_values = jnp.einsum("ij,fzjx->fzix", matrix, cube_values, precision=highest)
    cube_values = jnp.einsum("ij,fzyj->fzyi", matrix, cube_values, precision=highest)
    return cube_values.reshape(members, extent, plane_cells)


def kinetic_term(matrix, box_values):
    members, extent, plane_cells = box_values.shape
    cube_values = box_values.reshape(members, extent, extent, extent)
    along_planes = jnp.einsum("ij,fjyx->fiyx", matrix, cube_values, precision=highest)
    along_rows = jnp.einsum("ij,fzjx->fzix", matrix, cube_values, precision=highest)
    along_columns = jnp.einsum("ij,fzyj->fzyi", matrix, cube_values, precision=highest)
    return (along_planes + along_rows + along_columns).reshape(members, extent, plane_cells)


def potential_of(external, rho_values):
    return (external.astype(jnp.float32) - jnp.cbrt(3.0 / math.pi * rho_values)).astype(
        jnp.bfloat16
    )


def placement(starts, extent, edge):
    grid_index = jnp.arange(edge)[None, :, None]
    box_index = jnp.arange(extent)[None, None, :]
    target = jnp.mod(starts[:, None, None] + box_index, edge)
    return (grid_index == target).astype(jnp.float32)


def on_device(coefficients, box_offset, occupation, external_potential, core_density):
    members, extent, box_cells = coefficients.shape
    slab_rows, grid_cells = external_potential.shape
    regions = lax.axis_size("region")
    groups = lax.axis_size("group")
    grid_edge = math.isqrt(grid_cells)
    total_planes = slab_rows * regions
    reach_regions = extent // (2 * slab_rows)
    slot_count = 2 * reach_regions + 1
    coverage = float(total_planes * grid_cells) / float(members * regions * groups * extent**3)
    weight = coverage * occupation[0]
    synthesis = filter_matrix(extent)
    kinetic_op = kinetic_matrix(extent)
    base_plane = lax.axis_index("region") * slab_rows - reach_regions * slab_rows
    plane_shift = jnp.mod(box_offset[0, 0] - base_plane, total_planes)
    places = jnp.stack([box_offset[1, 0], box_offset[2, 0]]).astype(jnp.float32)
    offsets = [slot - reach_regions for slot in range(slot_count)]
    current = coefficients
    rho_values = None
    for sweep_index in range(STEPS):
        orbital = separable(synthesis, current)
        kinetic_part = kinetic_term(kinetic_op, current)
        weighted = weight * orbital[0] * orbital[0]
        padded = jnp.zeros((slot_count * slab_rows, box_cells), jnp.float32)
        padded = lax.dynamic_update_slice_in_dim(padded, weighted, plane_shift, 0)
        slots = padded.reshape(slot_count, slab_rows, box_cells)
        pieces, piece_places = [], []
        for slot_index, by in enumerate(offsets):
            if by == 0:
                got_piece, got_places = slots[slot_index], places
            else:
                got_piece, got_places = passed_along((slots[slot_index], places), "region", by)
            pieces.append(got_piece)
            piece_places.append(got_places)
        held = jnp.stack(pieces).reshape(slot_count, slab_rows, extent, extent)
        held_places = jnp.stack(piece_places).astype(jnp.int32)
        rows_onehot = placement(held_places[:, 0], extent, grid_edge)
        cols_onehot = placement(held_places[:, 1], extent, grid_edge)
        column_placed = jnp.einsum("kpij,kgj->kpig", held, cols_onehot, precision=highest)
        partial_slab = jnp.einsum(
            "khi,kpig->phg", rows_onehot, column_placed, precision=highest
        ).reshape(slab_rows, grid_cells)
        density = lax.psum(partial_slab, "group") + core_density
        if sweep_index == STEPS - 1:
            rho_values = density
        potential = potential_of(external_potential, density).reshape(
            slab_rows, grid_edge, grid_edge
        )
        rows_cut = rows_onehot.astype(jnp.bfloat16)
        cols_cut = cols_onehot.astype(jnp.bfloat16)
        row_windows = jnp.einsum(
            "khi,phg->kpig", rows_cut, potential, preferred_element_type=jnp.float32
        ).astype(jnp.bfloat16)
        cut = jnp.einsum(
            "kpig,kgj->kpij", row_windows, cols_cut, preferred_element_type=jnp.float32
        ).astype(jnp.bfloat16)
        cut = cut.reshape(slot_count, slab_rows, box_cells)
        returned = []
        for slot_index, by in enumerate(offsets):
            window_piece = cut[slot_index]
            if by != 0:
                window_piece = passed_along(window_piece, "region", -by)
            returned.append(window_piece)
        stacked = jnp.concatenate(returned, axis=0)
        windows = lax.dynamic_slice_in_dim(stacked, plane_shift, extent, 0).astype(jnp.float32)
        gradient = kinetic_part + separable(synthesis.T, windows[None] * orbital)
        current = current - step_size * gradient
    return (current, rho_values)


def solution(mesh):
    both = ("region", "group")
    return jax.shard_map(
        on_device,
        mesh=mesh,
        in_specs=(
            P(both, None, None),
            P(None, both),
            P(both),
            P("region", None),
            P("region", None),
        ),
        out_specs=(P(both, None, None), P("region", None)),
        check_vma=False,
    )
```

```python
import math

import jax
import jax.numpy as jnp
from jax import lax
from jax.sharding import Mesh
from jax.sharding import PartitionSpec as P

STEPS = 2

step_size = 0.1
highest = lax.Precision.HIGHEST


def passed_along(value, axis, by):
    count = lax.axis_size(axis)
    return lax.ppermute(value, axis, [(i, (i + by) % count) for i in range(count)])


def filter_matrix(extent):
    offset_index = (jnp.arange(extent)[:, None] - jnp.arange(extent)[None, :] + 8).astype(
        jnp.float32
    )
    tap_grid = jnp.arange(16).astype(jnp.float32)
    tap_values = jnp.exp(-0.5 * ((tap_grid - 7.5) / 1.2) ** 2)
    norm_value = jnp.sqrt(jnp.sum(tap_values * tap_values))
    values = jnp.exp(-0.5 * ((offset_index - 7.5) / 1.2) ** 2) / norm_value
    inside = (offset_index >= 0.0) & (offset_index <= 15.0)
    return jnp.where(inside, values, 0.0)


def kinetic_matrix(extent):
    distance = jnp.arange(extent)[:, None] - jnp.arange(extent)[None, :]
    magnitude = jnp.abs(distance)
    parity = 1.0 - 2.0 * (magnitude % 2).astype(jnp.float32)
    spread = jnp.maximum(magnitude, 1).astype(jnp.float32)
    values = parity / (spread * spread)
    values = jnp.where(magnitude == 0, math.pi**2 / 6.0, values)
    return jnp.where(magnitude <= 14, values, 0.0)


def separable(matrix, box_values):
    members, extent, plane_cells = box_values.shape
    cube_values = box_values.reshape(members, extent, extent, extent)
    cube_values = jnp.einsum("ij,fjyx->fiyx", matrix, cube_values, precision=highest)
    cube_values = jnp.einsum("ij,fzjx->fzix", matrix, cube_values, precision=highest)
    cube_values = jnp.einsum("ij,fzyj->fzyi", matrix, cube_values, precision=highest)
    return cube_values.reshape(members, extent, plane_cells)


def kinetic_term(matrix, box_values):
    members, extent, plane_cells = box_values.shape
    cube_values = box_values.reshape(members, extent, extent, extent)
    along_planes = jnp.einsum("ij,fjyx->fiyx", matrix, cube_values, precision=highest)
    along_rows = jnp.einsum("ij,fzjx->fzix", matrix, cube_values, precision=highest)
    along_columns = jnp.einsum("ij,fzyj->fzyi", matrix, cube_values, precision=highest)
    return (along_planes + along_rows + along_columns).reshape(members, extent, plane_cells)


def potential_of(external, rho_values):
    return (external.astype(jnp.float32) - jnp.cbrt(3.0 / math.pi * rho_values)).astype(
        jnp.bfloat16
    )


def placement(starts, extent, edge):
    grid_index = jnp.arange(edge)[None, :, None]
    box_index = jnp.arange(extent)[None, None, :]
    target = jnp.mod(starts[:, None, None] + box_index, edge)
    return (grid_index == target).astype(jnp.float32)


def shifted(value, axis, by):
    count = lax.axis_size(axis)
    return lax.ppermute(value, axis, [(i, (i + by) % count) for i in range(count)])


def swapped(value, axis):
    return lax.all_to_all(value, axis, 0, 0, tiled=True)


def on_device(coefficients, box_offset, occupation, external_potential, core_density):
    members, extent, box_cells = coefficients.shape
    slab_rows, grid_cells = external_potential.shape
    rows_z, rows_y = lax.axis_size("rz"), lax.axis_size("ry")
    regions = rows_z * rows_y
    groups = lax.axis_size("group")
    grid_edge = math.isqrt(grid_cells)
    total_planes = slab_rows * regions
    reach_regions = extent // (2 * slab_rows)
    row_planes = rows_y * slab_rows
    coverage = float(total_planes * grid_cells) / float(members * regions * groups * extent**3)
    weight = coverage * occupation[0]
    synthesis = filter_matrix(extent)
    kinetic_op = kinetic_matrix(extent)
    y_index = lax.axis_index("ry")
    region_index = lax.axis_index("rz") * rows_y + y_index
    base_plane = region_index * slab_rows - reach_regions * slab_rows
    plane_shift = jnp.mod(box_offset[0, 0] - base_plane, total_planes)
    window_start = plane_shift + slab_rows * y_index
    places = jnp.stack([box_offset[1, 0], box_offset[2, 0]]).astype(jnp.float32)
    near_places = jnp.stack([shifted(places, "rz", 1), places, shifted(places, "rz", -1)])
    held_places = lax.all_gather(near_places, "ry").reshape(-1, 2).astype(jnp.int32)
    pieces_count = held_places.shape[0]
    rows_onehot = placement(held_places[:, 0], extent, grid_edge)
    cols_onehot = placement(held_places[:, 1], extent, grid_edge)
    rows_cut = rows_onehot.astype(jnp.bfloat16)
    cols_cut = cols_onehot.astype(jnp.bfloat16)
    share_width = grid_cells // groups
    share_start = lax.axis_index("group") * share_width
    core_piece = lax.dynamic_slice_in_dim(core_density, share_start, share_width, 1)
    current = coefficients
    rho_values = None
    for sweep_index in range(STEPS):
        orbital = separable(synthesis, current)
        kinetic_part = kinetic_term(kinetic_op, current)
        weighted = weight * orbital[0] * orbital[0]
        window = jnp.zeros((3 * row_planes, box_cells), jnp.float32)
        window = lax.dynamic_update_slice_in_dim(window, weighted, window_start, 0)
        parts = window.reshape(3, rows_y, slab_rows, box_cells)
        from_below = shifted(parts[2], "rz", 1)
        from_above = shifted(parts[0], "rz", -1)
        near = jnp.stack([from_below, parts[1], from_above], axis=1)
        held = swapped(near, "ry").reshape(pieces_count, slab_rows, extent, extent)
        column_placed = jnp.einsum("kpij,kgj->kpig", held, cols_onehot, precision=highest)
        partial_slab = jnp.einsum(
            "khi,kpig->phg", rows_onehot, column_placed, precision=highest
        ).reshape(slab_rows, groups, share_width)
        share_sum = jnp.sum(swapped(jnp.swapaxes(partial_slab, 0, 1), "group"), axis=0)
        density_piece = share_sum + core_piece
        if sweep_index == STEPS - 1:
            gathered = swapped(jnp.broadcast_to(density_piece, (groups, *density_piece.shape)), "group")
            rho_values = jnp.swapaxes(gathered, 0, 1).reshape(slab_rows, grid_cells)
            potential = potential_of(external_potential, rho_values)
        else:
            external_piece = lax.dynamic_slice_in_dim(external_potential, share_start, share_width, 1)
            potential_piece = potential_of(external_piece, density_piece)
            gathered = swapped(
                jnp.broadcast_to(potential_piece, (groups, *potential_piece.shape)), "group"
            )
            potential = jnp.swapaxes(gathered, 0, 1)
        potential = potential.reshape(slab_rows, grid_edge, grid_edge)
        row_windows = jnp.einsum(
            "khi,phg->kpig", rows_cut, potential, preferred_element_type=jnp.float32
        ).astype(jnp.bfloat16)
        cut = jnp.einsum(
            "kpig,kgj->kpij", row_windows, cols_cut, preferred_element_type=jnp.float32
        ).astype(jnp.bfloat16)
        cut = swapped(cut.reshape(rows_y, 3, slab_rows, box_cells), "ry")
        back_parts = jnp.stack(
            [shifted(cut[:, 2], "rz", 1), cut[:, 1], shifted(cut[:, 0], "rz", -1)]
        ).reshape(3 * row_planes, box_cells)
        windows = lax.dynamic_slice_in_dim(back_parts, window_start, extent, 0).astype(jnp.float32)
        gradient = kinetic_part + separable(synthesis.T, windows[None] * orbital)
        current = current - step_size * gradient
    return (current, rho_values)


def solution(mesh):
    regions = mesh.shape["region"]
    rows_y = 4 if regions % 4 == 0 else 1
    torus = Mesh(
        mesh.devices.reshape(regions // rows_y, rows_y, mesh.shape["group"]), ("rz", "ry", "group")
    )
    every = ("rz", "ry", "group")
    return jax.shard_map(
        on_device,
        mesh=torus,
        in_specs=(
            P(every, None, None),
            P(None, every),
            P(every),
            P(("rz", "ry"), None),
            P(("rz", "ry"), None),
        ),
        out_specs=(P(every, None, None), P(("rz", "ry"), None)),
        check_vma=False,
    )
```

```python
import math

import jax
import jax.numpy as jnp
from jax import lax
from jax.sharding import Mesh
from jax.sharding import PartitionSpec as P

STEPS = 2

step_size = 0.1
highest = lax.Precision.HIGHEST


def passed_along(value, axis, by):
    count = lax.axis_size(axis)
    return lax.ppermute(value, axis, [(i, (i + by) % count) for i in range(count)])


def filter_matrix(extent):
    offset_index = (jnp.arange(extent)[:, None] - jnp.arange(extent)[None, :] + 8).astype(
        jnp.float32
    )
    tap_grid = jnp.arange(16).astype(jnp.float32)
    tap_values = jnp.exp(-0.5 * ((tap_grid - 7.5) / 1.2) ** 2)
    norm_value = jnp.sqrt(jnp.sum(tap_values * tap_values))
    values = jnp.exp(-0.5 * ((offset_index - 7.5) / 1.2) ** 2) / norm_value
    inside = (offset_index >= 0.0) & (offset_index <= 15.0)
    return jnp.where(inside, values, 0.0)


def kinetic_matrix(extent):
    distance = jnp.arange(extent)[:, None] - jnp.arange(extent)[None, :]
    magnitude = jnp.abs(distance)
    parity = 1.0 - 2.0 * (magnitude % 2).astype(jnp.float32)
    spread = jnp.maximum(magnitude, 1).astype(jnp.float32)
    values = parity / (spread * spread)
    values = jnp.where(magnitude == 0, math.pi**2 / 6.0, values)
    return jnp.where(magnitude <= 14, values, 0.0)


def separable(matrix, box_values):
    members, extent, plane_cells = box_values.shape
    cube_values = box_values.reshape(members, extent, extent, extent)
    cube_values = jnp.einsum("ij,fjyx->fiyx", matrix, cube_values, precision=highest)
    cube_values = jnp.einsum("ij,fzjx->fzix", matrix, cube_values, precision=highest)
    cube_values = jnp.einsum("ij,fzyj->fzyi", matrix, cube_values, precision=highest)
    return cube_values.reshape(members, extent, plane_cells)


def kinetic_term(matrix, box_values):
    members, extent, plane_cells = box_values.shape
    cube_values = box_values.reshape(members, extent, extent, extent)
    along_planes = jnp.einsum("ij,fjyx->fiyx", matrix, cube_values, precision=highest)
    along_rows = jnp.einsum("ij,fzjx->fzix", matrix, cube_values, precision=highest)
    along_columns = jnp.einsum("ij,fzyj->fzyi", matrix, cube_values, precision=highest)
    return (along_planes + along_rows + along_columns).reshape(members, extent, plane_cells)


def potential_of(external, rho_values):
    return (external.astype(jnp.float32) - jnp.cbrt(3.0 / math.pi * rho_values)).astype(
        jnp.bfloat16
    )


def placement(starts, extent, edge):
    grid_index = jnp.arange(edge)[None, :, None]
    box_index = jnp.arange(extent)[None, None, :]
    target = jnp.mod(starts[:, None, None] + box_index, edge)
    return (grid_index == target).astype(jnp.float32)


def shifted(value, axis, by):
    count = lax.axis_size(axis)
    return lax.ppermute(value, axis, [(i, (i + by) % count) for i in range(count)])


def swapped(value, axis):
    return lax.all_to_all(value, axis, 0, 0, tiled=True)


def on_device(coefficients, box_offset, occupation, external_potential, core_density):
    members, extent, box_cells = coefficients.shape
    slab_rows, grid_cells = external_potential.shape
    rows_z, rows_y = lax.axis_size("rz"), lax.axis_size("ry")
    regions = rows_z * rows_y
    groups = lax.axis_size("group")
    grid_edge = math.isqrt(grid_cells)
    total_planes = slab_rows * regions
    reach_regions = extent // (2 * slab_rows)
    row_planes = rows_y * slab_rows
    coverage = float(total_planes * grid_cells) / float(members * regions * groups * extent**3)
    weight = coverage * occupation[0]
    synthesis = filter_matrix(extent)
    kinetic_op = kinetic_matrix(extent)
    y_index = lax.axis_index("ry")
    region_index = lax.axis_index("rz") * rows_y + y_index
    base_plane = region_index * slab_rows - reach_regions * slab_rows
    plane_shift = jnp.mod(box_offset[0, 0] - base_plane, total_planes)
    window_start = plane_shift + slab_rows * y_index
    places = jnp.stack([box_offset[1, 0], box_offset[2, 0]]).astype(jnp.float32)
    near_places = jnp.stack([shifted(places, "rz", 1), places, shifted(places, "rz", -1)])
    pieces_count = 3 * rows_y
    piece_cells = slab_rows * box_cells
    place_lanes = 128
    near_places = jnp.pad(near_places, ((0, 0), (0, place_lanes - 2)))
    share_width = grid_cells // groups
    share_start = lax.axis_index("group") * share_width
    core_piece = lax.dynamic_slice_in_dim(core_density, share_start, share_width, 1)
    current = coefficients
    rho_values = None
    for sweep_index in range(STEPS):
        orbital = separable(synthesis, current)
        kinetic_part = kinetic_term(kinetic_op, current)
        weighted = weight * orbital[0] * orbital[0]
        window = jnp.zeros((3 * row_planes, box_cells), jnp.float32)
        window = lax.dynamic_update_slice_in_dim(window, weighted, window_start, 0)
        parts = window.reshape(3, rows_y, slab_rows, box_cells)
        from_below = shifted(parts[2], "rz", 1)
        from_above = shifted(parts[0], "rz", -1)
        near = jnp.stack([from_below, parts[1], from_above], axis=1)
        if sweep_index == 0:
            near = jnp.concatenate(
                [
                    near.reshape(rows_y, 3, piece_cells),
                    jnp.broadcast_to(near_places, (rows_y, 3, place_lanes)),
                ],
                axis=2,
            )
            held_all = swapped(near, "ry").reshape(pieces_count, piece_cells + place_lanes)
            held_places = held_all[:, piece_cells : piece_cells + 2].astype(jnp.int32)
            held = held_all[:, :piece_cells]
            rows_onehot = placement(held_places[:, 0], extent, grid_edge)
            cols_onehot = placement(held_places[:, 1], extent, grid_edge)
            rows_cut = rows_onehot.astype(jnp.bfloat16)
            cols_cut = cols_onehot.astype(jnp.bfloat16)
        else:
            held = swapped(near, "ry")
        held = held.reshape(pieces_count, slab_rows, extent, extent)
        column_placed = jnp.einsum("kpij,kgj->kpig", held, cols_onehot, precision=highest)
        partial_slab = jnp.einsum(
            "khi,kpig->phg", rows_onehot, column_placed, precision=highest
        ).reshape(slab_rows, groups, share_width)
        share_sum = jnp.sum(swapped(jnp.swapaxes(partial_slab, 0, 1), "group"), axis=0)
        density_piece = share_sum + core_piece
        if sweep_index == STEPS - 1:
            gathered = swapped(jnp.broadcast_to(density_piece, (groups, *density_piece.shape)), "group")
            rho_values = jnp.swapaxes(gathered, 0, 1).reshape(slab_rows, grid_cells)
        external_piece = lax.dynamic_slice_in_dim(external_potential, share_start, share_width, 1)
        potential_piece = potential_of(external_piece, density_piece)
        gathered = swapped(
            jnp.broadcast_to(potential_piece, (groups, *potential_piece.shape)), "group"
        )
        potential = jnp.swapaxes(gathered, 0, 1)
        potential = potential.reshape(slab_rows, grid_edge, grid_edge)
        row_windows = jnp.einsum(
            "khi,phg->kpig", rows_cut, potential, preferred_element_type=jnp.float32
        ).astype(jnp.bfloat16)
        cut = jnp.einsum(
            "kpig,kgj->kpij", row_windows, cols_cut, preferred_element_type=jnp.float32
        ).astype(jnp.bfloat16)
        cut = swapped(cut.reshape(rows_y, 3, slab_rows, box_cells), "ry")
        back_parts = jnp.stack(
            [shifted(cut[:, 2], "rz", 1), cut[:, 1], shifted(cut[:, 0], "rz", -1)]
        ).reshape(3 * row_planes, box_cells)
        windows = lax.dynamic_slice_in_dim(back_parts, window_start, extent, 0).astype(jnp.float32)
        gradient = kinetic_part + separable(synthesis.T, windows[None] * orbital)
        current = current - step_size * gradient
    return (current, rho_values)


def solution(mesh):
    regions = mesh.shape["region"]
    rows_y = 4 if regions % 4 == 0 else 1
    torus = Mesh(
        mesh.devices.reshape(regions // rows_y, rows_y, mesh.shape["group"]), ("rz", "ry", "group")
    )
    every = ("rz", "ry", "group")
    return jax.shard_map(
        on_device,
        mesh=torus,
        in_specs=(
            P(every, None, None),
            P(None, every),
            P(every),
            P(("rz", "ry"), None),
            P(("rz", "ry"), None),
        ),
        out_specs=(P(every, None, None), P(("rz", "ry"), None)),
        check_vma=False,
    )
```

```python
import math

import jax
import jax.numpy as jnp
from jax import lax
from jax.sharding import Mesh
from jax.sharding import PartitionSpec as P

STEPS = 2

step_size = 0.1
highest = lax.Precision.HIGHEST


def passed_along(value, axis, by):
    count = lax.axis_size(axis)
    return lax.ppermute(value, axis, [(i, (i + by) % count) for i in range(count)])


def filter_matrix(extent):
    offset_index = (jnp.arange(extent)[:, None] - jnp.arange(extent)[None, :] + 8).astype(
        jnp.float32
    )
    tap_grid = jnp.arange(16).astype(jnp.float32)
    tap_values = jnp.exp(-0.5 * ((tap_grid - 7.5) / 1.2) ** 2)
    norm_value = jnp.sqrt(jnp.sum(tap_values * tap_values))
    values = jnp.exp(-0.5 * ((offset_index - 7.5) / 1.2) ** 2) / norm_value
    inside = (offset_index >= 0.0) & (offset_index <= 15.0)
    return jnp.where(inside, values, 0.0)


def kinetic_matrix(extent):
    distance = jnp.arange(extent)[:, None] - jnp.arange(extent)[None, :]
    magnitude = jnp.abs(distance)
    parity = 1.0 - 2.0 * (magnitude % 2).astype(jnp.float32)
    spread = jnp.maximum(magnitude, 1).astype(jnp.float32)
    values = parity / (spread * spread)
    values = jnp.where(magnitude == 0, math.pi**2 / 6.0, values)
    return jnp.where(magnitude <= 14, values, 0.0)


def separable(matrix, box_values):
    members, extent, plane_cells = box_values.shape
    cube_values = box_values.reshape(members, extent, extent, extent)
    cube_values = jnp.einsum("ij,fjyx->fiyx", matrix, cube_values, precision=highest)
    cube_values = jnp.einsum("ij,fzjx->fzix", matrix, cube_values, precision=highest)
    cube_values = jnp.einsum("ij,fzyj->fzyi", matrix, cube_values, precision=highest)
    return cube_values.reshape(members, extent, plane_cells)


def kinetic_term(matrix, box_values):
    members, extent, plane_cells = box_values.shape
    cube_values = box_values.reshape(members, extent, extent, extent)
    along_planes = jnp.einsum("ij,fjyx->fiyx", matrix, cube_values, precision=highest)
    along_rows = jnp.einsum("ij,fzjx->fzix", matrix, cube_values, precision=highest)
    along_columns = jnp.einsum("ij,fzyj->fzyi", matrix, cube_values, precision=highest)
    return (along_planes + along_rows + along_columns).reshape(members, extent, plane_cells)


def potential_of(external, rho_values):
    return (external.astype(jnp.float32) - jnp.cbrt(3.0 / math.pi * rho_values)).astype(
        jnp.bfloat16
    )


def placement(starts, extent, edge):
    grid_index = jnp.arange(edge)[None, :, None]
    box_index = jnp.arange(extent)[None, None, :]
    target = jnp.mod(starts[:, None, None] + box_index, edge)
    return (grid_index == target).astype(jnp.float32)


def shifted(value, axis, by):
    count = lax.axis_size(axis)
    return lax.ppermute(value, axis, [(i, (i + by) % count) for i in range(count)])


def swapped(value, axis):
    return lax.all_to_all(value, axis, 0, 0, tiled=True)


def on_device(coefficients, box_offset, occupation, external_potential, core_density):
    members, extent, box_cells = coefficients.shape
    slab_rows, grid_cells = external_potential.shape
    rows_z, rows_y = lax.axis_size("rz"), lax.axis_size("ry")
    regions = rows_z * rows_y
    groups = lax.axis_size("group")
    grid_edge = math.isqrt(grid_cells)
    total_planes = slab_rows * regions
    reach_regions = extent // (2 * slab_rows)
    row_planes = rows_y * slab_rows
    coverage = float(total_planes * grid_cells) / float(members * regions * groups * extent**3)
    weight = coverage * occupation[0]
    synthesis = filter_matrix(extent)
    kinetic_op = kinetic_matrix(extent)
    y_index = lax.axis_index("ry")
    region_index = lax.axis_index("rz") * rows_y + y_index
    base_plane = region_index * slab_rows - reach_regions * slab_rows
    plane_shift = jnp.mod(box_offset[0, 0] - base_plane, total_planes)
    window_start = plane_shift + slab_rows * y_index
    owned_plane = jnp.minimum(lax.axis_index("group"), slab_rows - 1)
    core_plane = lax.dynamic_index_in_dim(core_density, owned_plane, 0, keepdims=False)
    external_plane = lax.dynamic_index_in_dim(external_potential, owned_plane, 0, keepdims=False)
    places = jnp.stack([box_offset[1, 0], box_offset[2, 0]]).astype(jnp.float32)
    near_places = jnp.stack([shifted(places, "rz", 1), places, shifted(places, "rz", -1)])
    place_lanes = 128
    near_places = jnp.pad(near_places, ((0, 0), (0, place_lanes - 2)))
    spread = ("ry", "group")
    pieces_count = 3 * rows_y * groups
    idle = groups - slab_rows
    current = coefficients
    rho_values = None
    for sweep_index in range(STEPS):
        orbital = separable(synthesis, current)
        kinetic_part = kinetic_term(kinetic_op, current)
        weighted = weight * orbital[0] * orbital[0]
        window = jnp.zeros((3 * row_planes, box_cells), jnp.float32)
        window = lax.dynamic_update_slice_in_dim(window, weighted, window_start, 0)
        parts = window.reshape(3, rows_y, slab_rows, box_cells)
        from_below = shifted(parts[2], "rz", 1)
        from_above = shifted(parts[0], "rz", -1)
        near = jnp.stack([from_below, parts[1], from_above], axis=2)
        near = jnp.pad(near, ((0, 0), (0, idle), (0, 0), (0, 0)))
        if sweep_index == 0:
            near = jnp.concatenate(
                [near, jnp.broadcast_to(near_places, (rows_y, groups, 3, place_lanes))], axis=3
            )
            held_all = swapped(near.reshape(rows_y * groups, 3, -1), spread)
            held_all = held_all.reshape(pieces_count, box_cells + place_lanes)
            held_places = held_all[:, box_cells : box_cells + 2].astype(jnp.int32)
            held = held_all[:, :box_cells]
            rows_onehot = placement(held_places[:, 0], extent, grid_edge)
            cols_onehot = placement(held_places[:, 1], extent, grid_edge)
            rows_cut = rows_onehot.astype(jnp.bfloat16)
            cols_cut = cols_onehot.astype(jnp.bfloat16)
        else:
            held = swapped(near.reshape(rows_y * groups, 3, box_cells), spread)
        held = held.reshape(pieces_count, extent, extent)
        column_placed = jnp.einsum("kij,kgj->kig", held, cols_onehot, precision=highest)
        plane_sum = jnp.einsum(
            "khi,kig->hg", rows_onehot, column_placed, precision=highest
        ).reshape(grid_cells)
        density_plane = plane_sum + core_plane
        if sweep_index == STEPS - 1:
            gathered = swapped(jnp.broadcast_to(density_plane, (groups, grid_cells)), "group")
            rho_values = gathered[:slab_rows]
        potential = potential_of(external_plane, density_plane).reshape(grid_edge, grid_edge)
        row_windows = jnp.einsum(
            "khi,hg->kig", rows_cut, potential, preferred_element_type=jnp.float32
        ).astype(jnp.bfloat16)
        cut = jnp.einsum(
            "kig,kgj->kij", row_windows, cols_cut, preferred_element_type=jnp.float32
        ).astype(jnp.bfloat16)
        cut = swapped(cut.reshape(rows_y * groups, 3, box_cells), spread)
        cut = cut.reshape(rows_y, groups, 3, box_cells)[:, :slab_rows]
        cut = jnp.swapaxes(cut, 1, 2)
        back_parts = jnp.stack(
            [shifted(cut[:, 2], "rz", 1), cut[:, 1], shifted(cut[:, 0], "rz", -1)]
        ).reshape(3 * row_planes, box_cells)
        windows = lax.dynamic_slice_in_dim(back_parts, window_start, extent, 0).astype(jnp.float32)
        gradient = kinetic_part + separable(synthesis.T, windows[None] * orbital)
        current = current - step_size * gradient
    return (current, rho_values)


def solution(mesh):
    regions = mesh.shape["region"]
    rows_y = 4 if regions % 4 == 0 else 1
    torus = Mesh(
        mesh.devices.reshape(regions // rows_y, rows_y, mesh.shape["group"]), ("rz", "ry", "group")
    )
    every = ("rz", "ry", "group")
    return jax.shard_map(
        on_device,
        mesh=torus,
        in_specs=(
            P(every, None, None),
            P(None, every),
            P(every),
            P(("rz", "ry"), None),
            P(("rz", "ry"), None),
        ),
        out_specs=(P(every, None, None), P(("rz", "ry"), None)),
        check_vma=False,
    )
```

```python
import math

import jax
import jax.numpy as jnp
from jax import lax
from jax.sharding import Mesh
from jax.sharding import PartitionSpec as P

STEPS = 2

step_size = 0.1
matmul_precision = lax.Precision.HIGH


def passed_along(value, axis, by):
    count = lax.axis_size(axis)
    return lax.ppermute(value, axis, [(i, (i + by) % count) for i in range(count)])


def filter_matrix(extent):
    offset_index = (jnp.arange(extent)[:, None] - jnp.arange(extent)[None, :] + 8).astype(
        jnp.float32
    )
    tap_grid = jnp.arange(16).astype(jnp.float32)
    tap_values = jnp.exp(-0.5 * ((tap_grid - 7.5) / 1.2) ** 2)
    norm_value = jnp.sqrt(jnp.sum(tap_values * tap_values))
    values = jnp.exp(-0.5 * ((offset_index - 7.5) / 1.2) ** 2) / norm_value
    inside = (offset_index >= 0.0) & (offset_index <= 15.0)
    return jnp.where(inside, values, 0.0)


def kinetic_matrix(extent):
    distance = jnp.arange(extent)[:, None] - jnp.arange(extent)[None, :]
    magnitude = jnp.abs(distance)
    parity = 1.0 - 2.0 * (magnitude % 2).astype(jnp.float32)
    spread = jnp.maximum(magnitude, 1).astype(jnp.float32)
    values = parity / (spread * spread)
    values = jnp.where(magnitude == 0, math.pi**2 / 6.0, values)
    return jnp.where(magnitude <= 14, values, 0.0)


def separable(matrix, box_values):
    members, extent, plane_cells = box_values.shape
    cube_values = box_values.reshape(members, extent, extent, extent)
    cube_values = jnp.einsum("ij,fjyx->fiyx", matrix, cube_values, precision=matmul_precision)
    cube_values = jnp.einsum("ij,fzjx->fzix", matrix, cube_values, precision=matmul_precision)
    cube_values = jnp.einsum("ij,fzyj->fzyi", matrix, cube_values, precision=matmul_precision)
    return cube_values.reshape(members, extent, plane_cells)


def kinetic_term(matrix, box_values):
    members, extent, plane_cells = box_values.shape
    cube_values = box_values.reshape(members, extent, extent, extent)
    along_planes = jnp.einsum("ij,fjyx->fiyx", matrix, cube_values, precision=matmul_precision)
    along_rows = jnp.einsum("ij,fzjx->fzix", matrix, cube_values, precision=matmul_precision)
    along_columns = jnp.einsum("ij,fzyj->fzyi", matrix, cube_values, precision=matmul_precision)
    return (along_planes + along_rows + along_columns).reshape(members, extent, plane_cells)


def potential_of(external, rho_values):
    return (external.astype(jnp.float32) - jnp.cbrt(3.0 / math.pi * rho_values)).astype(
        jnp.bfloat16
    )


def placement(starts, extent, edge):
    grid_index = jnp.arange(edge)[None, :, None]
    box_index = jnp.arange(extent)[None, None, :]
    target = jnp.mod(starts[:, None, None] + box_index, edge)
    return (grid_index == target).astype(jnp.float32)


def shifted(value, axis, by):
    count = lax.axis_size(axis)
    return lax.ppermute(value, axis, [(i, (i + by) % count) for i in range(count)])


def swapped(value, axis):
    return lax.all_to_all(value, axis, 0, 0, tiled=True)


def on_device(coefficients, box_offset, occupation, external_potential, core_density):
    members, extent, box_cells = coefficients.shape
    slab_rows, grid_cells = external_potential.shape
    rows_z, rows_y = lax.axis_size("rz"), lax.axis_size("ry")
    regions = rows_z * rows_y
    groups = lax.axis_size("group")
    grid_edge = math.isqrt(grid_cells)
    total_planes = slab_rows * regions
    reach_regions = extent // (2 * slab_rows)
    row_planes = rows_y * slab_rows
    coverage = float(total_planes * grid_cells) / float(members * regions * groups * extent**3)
    weight = coverage * occupation[0]
    synthesis = filter_matrix(extent)
    kinetic_op = kinetic_matrix(extent)
    y_index = lax.axis_index("ry")
    region_index = lax.axis_index("rz") * rows_y + y_index
    base_plane = region_index * slab_rows - reach_regions * slab_rows
    plane_shift = jnp.mod(box_offset[0, 0] - base_plane, total_planes)
    window_start = plane_shift + slab_rows * y_index
    owned_plane = jnp.minimum(lax.axis_index("group"), slab_rows - 1)
    core_plane = lax.dynamic_index_in_dim(core_density, owned_plane, 0, keepdims=False)
    external_plane = lax.dynamic_index_in_dim(external_potential, owned_plane, 0, keepdims=False)
    places = jnp.stack([box_offset[1, 0], box_offset[2, 0]]).astype(jnp.float32)
    near_places = jnp.stack([shifted(places, "rz", 1), places, shifted(places, "rz", -1)])
    place_lanes = 128
    near_places = jnp.pad(near_places, ((0, 0), (0, place_lanes - 2)))
    spread = ("ry", "group")
    pieces_count = 3 * rows_y * groups
    idle = groups - slab_rows
    current = coefficients
    rho_values = None
    for sweep_index in range(STEPS):
        orbital = separable(synthesis, current)
        kinetic_part = kinetic_term(kinetic_op, current)
        weighted = weight * orbital[0] * orbital[0]
        window = jnp.zeros((3 * row_planes, box_cells), jnp.float32)
        window = lax.dynamic_update_slice_in_dim(window, weighted, window_start, 0)
        parts = window.reshape(3, rows_y, slab_rows, box_cells)
        from_below = shifted(parts[2], "rz", 1)
        from_above = shifted(parts[0], "rz", -1)
        near = jnp.stack([from_below, parts[1], from_above], axis=2)
        near = jnp.pad(near, ((0, 0), (0, idle), (0, 0), (0, 0)))
        if sweep_index == 0:
            near = jnp.concatenate(
                [near, jnp.broadcast_to(near_places, (rows_y, groups, 3, place_lanes))], axis=3
            )
            held_all = swapped(near.reshape(rows_y * groups, 3, -1), spread)
            held_all = held_all.reshape(pieces_count, box_cells + place_lanes)
            held_places = held_all[:, box_cells : box_cells + 2].astype(jnp.int32)
            held = held_all[:, :box_cells]
            rows_onehot = placement(held_places[:, 0], extent, grid_edge)
            cols_onehot = placement(held_places[:, 1], extent, grid_edge)
            rows_cut = rows_onehot.astype(jnp.bfloat16)
            cols_cut = cols_onehot.astype(jnp.bfloat16)
        else:
            held = swapped(near.reshape(rows_y * groups, 3, box_cells), spread)
        held = held.reshape(pieces_count, extent, extent)
        column_placed = jnp.einsum("kij,kgj->kig", held, cols_onehot, precision=matmul_precision)
        plane_sum = jnp.einsum(
            "khi,kig->hg", rows_onehot, column_placed, precision=matmul_precision
        ).reshape(grid_cells)
        density_plane = plane_sum + core_plane
        if sweep_index == STEPS - 1:
            gathered = swapped(jnp.broadcast_to(density_plane, (groups, grid_cells)), "group")
            rho_values = gathered[:slab_rows]
        potential = potential_of(external_plane, density_plane).reshape(grid_edge, grid_edge)
        row_windows = jnp.einsum(
            "khi,hg->kig", rows_cut, potential, preferred_element_type=jnp.float32
        ).astype(jnp.bfloat16)
        cut = jnp.einsum(
            "kig,kgj->kij", row_windows, cols_cut, preferred_element_type=jnp.float32
        ).astype(jnp.bfloat16)
        cut = swapped(cut.reshape(rows_y * groups, 3, box_cells), spread)
        cut = cut.reshape(rows_y, groups, 3, box_cells)[:, :slab_rows]
        cut = jnp.swapaxes(cut, 1, 2)
        back_parts = jnp.stack(
            [shifted(cut[:, 2], "rz", 1), cut[:, 1], shifted(cut[:, 0], "rz", -1)]
        ).reshape(3 * row_planes, box_cells)
        windows = lax.dynamic_slice_in_dim(back_parts, window_start, extent, 0).astype(jnp.float32)
        gradient = kinetic_part + separable(synthesis.T, windows[None] * orbital)
        current = current - step_size * gradient
    return (current, rho_values)


def solution(mesh):
    regions = mesh.shape["region"]
    rows_y = 4 if regions % 4 == 0 else 1
    torus = Mesh(
        mesh.devices.reshape(regions // rows_y, rows_y, mesh.shape["group"]), ("rz", "ry", "group")
    )
    every = ("rz", "ry", "group")
    return jax.shard_map(
        on_device,
        mesh=torus,
        in_specs=(
            P(every, None, None),
            P(None, every),
            P(every),
            P(("rz", "ry"), None),
            P(("rz", "ry"), None),
        ),
        out_specs=(P(every, None, None), P(("rz", "ry"), None)),
        check_vma=False,
    )
```

```python
import math

import jax
import jax.numpy as jnp
from jax import lax
from jax.sharding import Mesh
from jax.sharding import PartitionSpec as P

STEPS = 2

step_size = 0.1
matmul_precision = lax.Precision.HIGH
density_precision = lax.Precision.HIGHEST


def passed_along(value, axis, by):
    count = lax.axis_size(axis)
    return lax.ppermute(value, axis, [(i, (i + by) % count) for i in range(count)])


def filter_matrix(extent):
    offset_index = (jnp.arange(extent)[:, None] - jnp.arange(extent)[None, :] + 8).astype(
        jnp.float32
    )
    tap_grid = jnp.arange(16).astype(jnp.float32)
    tap_values = jnp.exp(-0.5 * ((tap_grid - 7.5) / 1.2) ** 2)
    norm_value = jnp.sqrt(jnp.sum(tap_values * tap_values))
    values = jnp.exp(-0.5 * ((offset_index - 7.5) / 1.2) ** 2) / norm_value
    inside = (offset_index >= 0.0) & (offset_index <= 15.0)
    return jnp.where(inside, values, 0.0)


def kinetic_matrix(extent):
    distance = jnp.arange(extent)[:, None] - jnp.arange(extent)[None, :]
    magnitude = jnp.abs(distance)
    parity = 1.0 - 2.0 * (magnitude % 2).astype(jnp.float32)
    spread = jnp.maximum(magnitude, 1).astype(jnp.float32)
    values = parity / (spread * spread)
    values = jnp.where(magnitude == 0, math.pi**2 / 6.0, values)
    return jnp.where(magnitude <= 14, values, 0.0)


def separable(matrix, box_values, precision=matmul_precision):
    members, extent, plane_cells = box_values.shape
    cube_values = box_values.reshape(members, extent, extent, extent)
    cube_values = jnp.einsum("ij,fjyx->fiyx", matrix, cube_values, precision=precision)
    cube_values = jnp.einsum("ij,fzjx->fzix", matrix, cube_values, precision=precision)
    cube_values = jnp.einsum("ij,fzyj->fzyi", matrix, cube_values, precision=precision)
    return cube_values.reshape(members, extent, plane_cells)


def kinetic_term(matrix, box_values):
    members, extent, plane_cells = box_values.shape
    cube_values = box_values.reshape(members, extent, extent, extent)
    along_planes = jnp.einsum("ij,fjyx->fiyx", matrix, cube_values, precision=matmul_precision)
    along_rows = jnp.einsum("ij,fzjx->fzix", matrix, cube_values, precision=matmul_precision)
    along_columns = jnp.einsum("ij,fzyj->fzyi", matrix, cube_values, precision=matmul_precision)
    return (along_planes + along_rows + along_columns).reshape(members, extent, plane_cells)


def potential_of(external, rho_values):
    return (external.astype(jnp.float32) - jnp.cbrt(3.0 / math.pi * rho_values)).astype(
        jnp.bfloat16
    )


def placement(starts, extent, edge):
    grid_index = jnp.arange(edge)[None, :, None]
    box_index = jnp.arange(extent)[None, None, :]
    target = jnp.mod(starts[:, None, None] + box_index, edge)
    return (grid_index == target).astype(jnp.float32)


def shifted(value, axis, by):
    count = lax.axis_size(axis)
    return lax.ppermute(value, axis, [(i, (i + by) % count) for i in range(count)])


def swapped(value, axis):
    return lax.all_to_all(value, axis, 0, 0, tiled=True)


def on_device(coefficients, box_offset, occupation, external_potential, core_density):
    members, extent, box_cells = coefficients.shape
    slab_rows, grid_cells = external_potential.shape
    rows_z, rows_y = lax.axis_size("rz"), lax.axis_size("ry")
    regions = rows_z * rows_y
    groups = lax.axis_size("group")
    grid_edge = math.isqrt(grid_cells)
    total_planes = slab_rows * regions
    reach_regions = extent // (2 * slab_rows)
    row_planes = rows_y * slab_rows
    coverage = float(total_planes * grid_cells) / float(members * regions * groups * extent**3)
    weight = coverage * occupation[0]
    synthesis = filter_matrix(extent)
    kinetic_op = kinetic_matrix(extent)
    y_index = lax.axis_index("ry")
    region_index = lax.axis_index("rz") * rows_y + y_index
    base_plane = region_index * slab_rows - reach_regions * slab_rows
    plane_shift = jnp.mod(box_offset[0, 0] - base_plane, total_planes)
    window_start = plane_shift + slab_rows * y_index
    owned_plane = jnp.minimum(lax.axis_index("group"), slab_rows - 1)
    core_plane = lax.dynamic_index_in_dim(core_density, owned_plane, 0, keepdims=False)
    external_plane = lax.dynamic_index_in_dim(external_potential, owned_plane, 0, keepdims=False)
    places = jnp.stack([box_offset[1, 0], box_offset[2, 0]]).astype(jnp.float32)
    near_places = jnp.stack([shifted(places, "rz", 1), places, shifted(places, "rz", -1)])
    place_lanes = 128
    near_places = jnp.pad(near_places, ((0, 0), (0, place_lanes - 2)))
    spread = ("ry", "group")
    pieces_count = 3 * rows_y * groups
    idle = groups - slab_rows
    current = coefficients
    rho_values = None
    for sweep_index in range(STEPS):
        orbital = separable(synthesis, current, density_precision)
        kinetic_part = kinetic_term(kinetic_op, current)
        weighted = weight * orbital[0] * orbital[0]
        window = jnp.zeros((3 * row_planes, box_cells), jnp.float32)
        window = lax.dynamic_update_slice_in_dim(window, weighted, window_start, 0)
        parts = window.reshape(3, rows_y, slab_rows, box_cells)
        from_below = shifted(parts[2], "rz", 1)
        from_above = shifted(parts[0], "rz", -1)
        near = jnp.stack([from_below, parts[1], from_above], axis=2)
        near = jnp.pad(near, ((0, 0), (0, idle), (0, 0), (0, 0)))
        if sweep_index == 0:
            near = jnp.concatenate(
                [near, jnp.broadcast_to(near_places, (rows_y, groups, 3, place_lanes))], axis=3
            )
            held_all = swapped(near.reshape(rows_y * groups, 3, -1), spread)
            held_all = held_all.reshape(pieces_count, box_cells + place_lanes)
            held_places = held_all[:, box_cells : box_cells + 2].astype(jnp.int32)
            held = held_all[:, :box_cells]
            rows_onehot = placement(held_places[:, 0], extent, grid_edge)
            cols_onehot = placement(held_places[:, 1], extent, grid_edge)
            rows_cut = rows_onehot.astype(jnp.bfloat16)
            cols_cut = cols_onehot.astype(jnp.bfloat16)
        else:
            held = swapped(near.reshape(rows_y * groups, 3, box_cells), spread)
        held = held.reshape(pieces_count, extent, extent)
        column_placed = jnp.einsum("kij,kgj->kig", held, cols_onehot, precision=density_precision)
        plane_sum = jnp.einsum(
            "khi,kig->hg", rows_onehot, column_placed, precision=density_precision
        ).reshape(grid_cells)
        density_plane = plane_sum + core_plane
        if sweep_index == STEPS - 1:
            gathered = swapped(jnp.broadcast_to(density_plane, (groups, grid_cells)), "group")
            rho_values = gathered[:slab_rows]
        potential = potential_of(external_plane, density_plane).reshape(grid_edge, grid_edge)
        row_windows = jnp.einsum(
            "khi,hg->kig", rows_cut, potential, preferred_element_type=jnp.float32
        ).astype(jnp.bfloat16)
        cut = jnp.einsum(
            "kig,kgj->kij", row_windows, cols_cut, preferred_element_type=jnp.float32
        ).astype(jnp.bfloat16)
        cut = swapped(cut.reshape(rows_y * groups, 3, box_cells), spread)
        cut = cut.reshape(rows_y, groups, 3, box_cells)[:, :slab_rows]
        cut = jnp.swapaxes(cut, 1, 2)
        back_parts = jnp.stack(
            [shifted(cut[:, 2], "rz", 1), cut[:, 1], shifted(cut[:, 0], "rz", -1)]
        ).reshape(3 * row_planes, box_cells)
        windows = lax.dynamic_slice_in_dim(back_parts, window_start, extent, 0).astype(jnp.float32)
        gradient = kinetic_part + separable(synthesis.T, windows[None] * orbital)
        current = current - step_size * gradient
    return (current, rho_values)


def solution(mesh):
    regions = mesh.shape["region"]
    rows_y = 4 if regions % 4 == 0 else 1
    torus = Mesh(
        mesh.devices.reshape(regions // rows_y, rows_y, mesh.shape["group"]), ("rz", "ry", "group")
    )
    every = ("rz", "ry", "group")
    return jax.shard_map(
        on_device,
        mesh=torus,
        in_specs=(
            P(every, None, None),
            P(None, every),
            P(every),
            P(("rz", "ry"), None),
            P(("rz", "ry"), None),
        ),
        out_specs=(P(every, None, None), P(("rz", "ry"), None)),
        check_vma=False,
    )
```

```python
import math

import jax
import numpy as np
import jax.numpy as jnp
from jax import lax
from jax.sharding import Mesh
from jax.sharding import PartitionSpec as P

STEPS = 2

step_size = 0.1
matmul_precision = lax.Precision.HIGH


def passed_along(value, axis, by):
    count = lax.axis_size(axis)
    return lax.ppermute(value, axis, [(i, (i + by) % count) for i in range(count)])


def filter_matrix(extent):
    offset_index = (np.arange(extent)[:, None] - np.arange(extent)[None, :] + 8).astype(np.float32)
    tap_grid = np.arange(16).astype(np.float32)
    tap_values = np.exp(-0.5 * ((tap_grid - 7.5) / 1.2) ** 2)
    norm_value = np.sqrt(np.sum(tap_values * tap_values))
    values = np.exp(-0.5 * ((offset_index - 7.5) / 1.2) ** 2) / norm_value
    inside = (offset_index >= 0.0) & (offset_index <= 15.0)
    return np.where(inside, values, 0.0).astype(np.float32)


def kinetic_matrix(extent):
    distance = np.arange(extent)[:, None] - np.arange(extent)[None, :]
    magnitude = np.abs(distance)
    parity = 1.0 - 2.0 * (magnitude % 2)
    spread = np.maximum(magnitude, 1).astype(np.float64)
    values = parity / (spread * spread)
    values = np.where(magnitude == 0, math.pi**2 / 6.0, values)
    return np.where(magnitude <= 14, values, 0.0).astype(np.float32)


def separable(matrix, box_values):
    members, extent, plane_cells = box_values.shape
    cube_values = box_values.reshape(members, extent, extent, extent)
    cube_values = jnp.einsum("ij,fjyx->fiyx", matrix, cube_values, precision=matmul_precision)
    cube_values = jnp.einsum("ij,fzjx->fzix", matrix, cube_values, precision=matmul_precision)
    cube_values = jnp.einsum("ij,fzyj->fzyi", matrix, cube_values, precision=matmul_precision)
    return cube_values.reshape(members, extent, plane_cells)


def kinetic_term(matrix, box_values):
    members, extent, plane_cells = box_values.shape
    cube_values = box_values.reshape(members, extent, extent, extent)
    along_planes = jnp.einsum("ij,fjyx->fiyx", matrix, cube_values, precision=matmul_precision)
    along_rows = jnp.einsum("ij,fzjx->fzix", matrix, cube_values, precision=matmul_precision)
    along_columns = jnp.einsum("ij,fzyj->fzyi", matrix, cube_values, precision=matmul_precision)
    return (along_planes + along_rows + along_columns).reshape(members, extent, plane_cells)


def potential_of(external, rho_values):
    return (external.astype(jnp.float32) - jnp.cbrt(3.0 / math.pi * rho_values)).astype(
        jnp.bfloat16
    )


def placement(starts, extent, edge):
    grid_index = jnp.arange(edge)[None, :, None]
    box_index = jnp.arange(extent)[None, None, :]
    target = jnp.mod(starts[:, None, None] + box_index, edge)
    return (grid_index == target).astype(jnp.float32)


def shifted(value, axis, by):
    count = lax.axis_size(axis)
    return lax.ppermute(value, axis, [(i, (i + by) % count) for i in range(count)])


def swapped(value, axis):
    return lax.all_to_all(value, axis, 0, 0, tiled=True)


def on_device(coefficients, box_offset, occupation, external_potential, core_density):
    members, extent, box_cells = coefficients.shape
    slab_rows, grid_cells = external_potential.shape
    rows_z, rows_y = lax.axis_size("rz"), lax.axis_size("ry")
    regions = rows_z * rows_y
    groups = lax.axis_size("group")
    grid_edge = math.isqrt(grid_cells)
    total_planes = slab_rows * regions
    reach_regions = extent // (2 * slab_rows)
    row_planes = rows_y * slab_rows
    coverage = float(total_planes * grid_cells) / float(members * regions * groups * extent**3)
    weight = coverage * occupation[0]
    synthesis = filter_matrix(extent)
    kinetic_op = kinetic_matrix(extent)
    y_index = lax.axis_index("ry")
    region_index = lax.axis_index("rz") * rows_y + y_index
    base_plane = region_index * slab_rows - reach_regions * slab_rows
    plane_shift = jnp.mod(box_offset[0, 0] - base_plane, total_planes)
    window_start = plane_shift + slab_rows * y_index
    owned_plane = jnp.minimum(lax.axis_index("group"), slab_rows - 1)
    core_plane = lax.dynamic_index_in_dim(core_density, owned_plane, 0, keepdims=False)
    external_plane = lax.dynamic_index_in_dim(external_potential, owned_plane, 0, keepdims=False)
    place_lanes = 128
    places = jnp.stack([box_offset[1, 0], box_offset[2, 0]]).astype(jnp.float32)
    places = jnp.pad(places, (0, place_lanes - 2))
    spread = ("ry", "group")
    pieces_count = 3 * rows_y * groups
    idle = groups - slab_rows
    current = coefficients
    rho_values = None
    for sweep_index in range(STEPS):
        orbital = separable(synthesis, current)
        kinetic_part = kinetic_term(kinetic_op, current)
        weighted = weight * orbital[0] * orbital[0]
        window = jnp.zeros((3 * row_planes, box_cells), jnp.float32)
        window = lax.dynamic_update_slice_in_dim(window, weighted, window_start, 0)
        parts = window.reshape(3, rows_y, slab_rows, box_cells)
        if sweep_index == 0:
            piece_cells = slab_rows * box_cells
            tagged = jnp.concatenate(
                [
                    parts[::2].reshape(2, rows_y, piece_cells),
                    jnp.broadcast_to(places, (2, rows_y, place_lanes)),
                ],
                axis=2,
            )
            got_below = shifted(tagged[1], "rz", 1)
            got_above = shifted(tagged[0], "rz", -1)
            from_below = got_below[:, :piece_cells].reshape(rows_y, slab_rows, box_cells)
            from_above = got_above[:, :piece_cells].reshape(rows_y, slab_rows, box_cells)
            near_places = jnp.stack([got_below[0, piece_cells:], places, got_above[0, piece_cells:]])
        else:
            from_below = shifted(parts[2], "rz", 1)
            from_above = shifted(parts[0], "rz", -1)
        near = jnp.stack([from_below, parts[1], from_above], axis=2)
        near = jnp.pad(near, ((0, 0), (0, idle), (0, 0), (0, 0)))
        if sweep_index == 0:
            near = jnp.concatenate(
                [near, jnp.broadcast_to(near_places, (rows_y, groups, 3, place_lanes))], axis=3
            )
            held_all = swapped(near.reshape(rows_y * groups, 3, -1), spread)
            held_all = held_all.reshape(pieces_count, box_cells + place_lanes)
            held_places = held_all[:, box_cells : box_cells + 2].astype(jnp.int32)
            held = held_all[:, :box_cells]
            rows_onehot = placement(held_places[:, 0], extent, grid_edge)
            cols_onehot = placement(held_places[:, 1], extent, grid_edge)
            rows_cut = rows_onehot.astype(jnp.bfloat16)
            cols_cut = cols_onehot.astype(jnp.bfloat16)
        else:
            held = swapped(near.reshape(rows_y * groups, 3, box_cells), spread)
        held = held.reshape(pieces_count, extent, extent)
        column_placed = jnp.einsum("kij,kgj->kig", held, cols_onehot, precision=matmul_precision)
        plane_sum = jnp.einsum(
            "khi,kig->hg", rows_onehot, column_placed, precision=matmul_precision
        ).reshape(grid_cells)
        density_plane = plane_sum + core_plane
        if sweep_index == STEPS - 1:
            gathered = swapped(jnp.broadcast_to(density_plane, (groups, grid_cells)), "group")
            rho_values = gathered[:slab_rows]
        potential = potential_of(external_plane, density_plane).reshape(grid_edge, grid_edge)
        row_windows = jnp.einsum(
            "khi,hg->kig", rows_cut, potential, preferred_element_type=jnp.float32
        ).astype(jnp.bfloat16)
        cut = jnp.einsum(
            "kig,kgj->kij", row_windows, cols_cut, preferred_element_type=jnp.float32
        ).astype(jnp.bfloat16)
        cut = swapped(cut.reshape(rows_y * groups, 3, box_cells), spread)
        cut = cut.reshape(rows_y, groups, 3, box_cells)[:, :slab_rows]
        cut = jnp.swapaxes(cut, 1, 2)
        back_parts = jnp.stack(
            [shifted(cut[:, 2], "rz", 1), cut[:, 1], shifted(cut[:, 0], "rz", -1)]
        ).reshape(3 * row_planes, box_cells)
        windows = lax.dynamic_slice_in_dim(back_parts, window_start, extent, 0).astype(jnp.float32)
        gradient = kinetic_part + separable(synthesis.T, windows[None] * orbital)
        current = current - step_size * gradient
    return (current, rho_values)


def solution(mesh):
    regions = mesh.shape["region"]
    rows_y = 4 if regions % 4 == 0 else 1
    torus = Mesh(
        mesh.devices.reshape(regions // rows_y, rows_y, mesh.shape["group"]), ("rz", "ry", "group")
    )
    every = ("rz", "ry", "group")
    return jax.shard_map(
        on_device,
        mesh=torus,
        in_specs=(
            P(every, None, None),
            P(None, every),
            P(every),
            P(("rz", "ry"), None),
            P(("rz", "ry"), None),
        ),
        out_specs=(P(every, None, None), P(("rz", "ry"), None)),
        check_vma=False,
    )
```

```python
import math

import jax
import numpy as np
import jax.numpy as jnp
from jax import lax
from jax.sharding import Mesh
from jax.sharding import PartitionSpec as P

STEPS = 2

step_size = 0.1
matmul_precision = lax.Precision.HIGH


def passed_along(value, axis, by):
    count = lax.axis_size(axis)
    return lax.ppermute(value, axis, [(i, (i + by) % count) for i in range(count)])


def filter_matrix(extent):
    offset_index = (np.arange(extent)[:, None] - np.arange(extent)[None, :] + 8).astype(np.float32)
    tap_grid = np.arange(16).astype(np.float32)
    tap_values = np.exp(-0.5 * ((tap_grid - 7.5) / 1.2) ** 2)
    norm_value = np.sqrt(np.sum(tap_values * tap_values))
    values = np.exp(-0.5 * ((offset_index - 7.5) / 1.2) ** 2) / norm_value
    inside = (offset_index >= 0.0) & (offset_index <= 15.0)
    return np.where(inside, values, 0.0).astype(np.float32)


def kinetic_matrix(extent):
    distance = np.arange(extent)[:, None] - np.arange(extent)[None, :]
    magnitude = np.abs(distance)
    parity = 1.0 - 2.0 * (magnitude % 2)
    spread = np.maximum(magnitude, 1).astype(np.float64)
    values = parity / (spread * spread)
    values = np.where(magnitude == 0, math.pi**2 / 6.0, values)
    return np.where(magnitude <= 14, values, 0.0).astype(np.float32)


def separable(matrix, box_values):
    members, extent, plane_cells = box_values.shape
    cube_values = box_values.reshape(members, extent, extent, extent)
    cube_values = jnp.einsum("ij,fjyx->fiyx", matrix, cube_values, precision=matmul_precision)
    cube_values = jnp.einsum("ij,fzjx->fzix", matrix, cube_values, precision=matmul_precision)
    cube_values = jnp.einsum("ij,fzyj->fzyi", matrix, cube_values, precision=matmul_precision)
    return cube_values.reshape(members, extent, plane_cells)


def kinetic_term(matrix, box_values):
    members, extent, plane_cells = box_values.shape
    cube_values = box_values.reshape(members, extent, extent, extent)
    along_planes = jnp.einsum("ij,fjyx->fiyx", matrix, cube_values, precision=matmul_precision)
    along_rows = jnp.einsum("ij,fzjx->fzix", matrix, cube_values, precision=matmul_precision)
    along_columns = jnp.einsum("ij,fzyj->fzyi", matrix, cube_values, precision=matmul_precision)
    return (along_planes + along_rows + along_columns).reshape(members, extent, plane_cells)


def potential_of(external, rho_values):
    return (external.astype(jnp.float32) - jnp.cbrt(3.0 / math.pi * rho_values)).astype(
        jnp.bfloat16
    )


def placement(starts, extent, edge):
    grid_index = jnp.arange(edge)[None, :, None]
    box_index = jnp.arange(extent)[None, None, :]
    target = jnp.mod(starts[:, None, None] + box_index, edge)
    return (grid_index == target).astype(jnp.float32)


def shifted(value, axis, by):
    count = lax.axis_size(axis)
    return lax.ppermute(value, axis, [(i, (i + by) % count) for i in range(count)])


def swapped(value, axis):
    return lax.all_to_all(value, axis, 0, 0, tiled=True)


def on_device(coefficients, box_offset, occupation, external_potential, core_density):
    members, extent, box_cells = coefficients.shape
    slab_rows, grid_cells = external_potential.shape
    rows_z, rows_y = lax.axis_size("rz"), lax.axis_size("ry")
    regions = rows_z * rows_y
    groups = lax.axis_size("group")
    grid_edge = math.isqrt(grid_cells)
    total_planes = slab_rows * regions
    reach_regions = extent // (2 * slab_rows)
    row_planes = rows_y * slab_rows
    coverage = float(total_planes * grid_cells) / float(members * regions * groups * extent**3)
    weight = coverage * occupation[0]
    synthesis = filter_matrix(extent)
    kinetic_op = kinetic_matrix(extent)
    y_index = lax.axis_index("ry")
    region_index = lax.axis_index("rz") * rows_y + y_index
    base_plane = region_index * slab_rows - reach_regions * slab_rows
    plane_shift = jnp.mod(box_offset[0, 0] - base_plane, total_planes)
    window_start = plane_shift + slab_rows * y_index
    owned_plane = jnp.minimum(lax.axis_index("group"), slab_rows - 1)
    core_plane = lax.dynamic_index_in_dim(core_density, owned_plane, 0, keepdims=False)
    external_plane = lax.dynamic_index_in_dim(external_potential, owned_plane, 0, keepdims=False)
    place_lanes = 128
    places = jnp.stack([box_offset[1, 0], box_offset[2, 0]]).astype(jnp.float32)
    places = jnp.pad(places, (0, place_lanes - 2))
    spread = ("ry", "group")
    pieces_count = 3 * rows_y * groups
    idle = groups - slab_rows
    current = coefficients
    rho_values = None
    for sweep_index in range(STEPS):
        orbital = separable(synthesis, current)
        kinetic_part = kinetic_term(kinetic_op, current)
        weighted = weight * orbital[0] * orbital[0]
        window = jnp.zeros((3 * row_planes, box_cells), jnp.float32)
        window = lax.dynamic_update_slice_in_dim(window, weighted, window_start, 0)
        parts = window.reshape(3, rows_y, slab_rows, box_cells)
        if sweep_index == 0:
            piece_cells = slab_rows * box_cells
            tagged = jnp.concatenate(
                [
                    parts[::2].reshape(2, rows_y, piece_cells),
                    jnp.broadcast_to(places, (2, rows_y, place_lanes)),
                ],
                axis=2,
            )
            got_below = shifted(tagged[1], "rz", 1)
            got_above = shifted(tagged[0], "rz", -1)
            from_below = got_below[:, :piece_cells].reshape(rows_y, slab_rows, box_cells)
            from_above = got_above[:, :piece_cells].reshape(rows_y, slab_rows, box_cells)
            near_places = jnp.stack([got_below[0, piece_cells:], places, got_above[0, piece_cells:]])
        else:
            from_below = shifted(parts[2], "rz", 1)
            from_above = shifted(parts[0], "rz", -1)
        near = jnp.stack([from_below, parts[1], from_above], axis=2)
        near = jnp.pad(near, ((0, 0), (0, idle), (0, 0), (0, 0)))
        if sweep_index == 0:
            near = jnp.concatenate(
                [near, jnp.broadcast_to(near_places, (rows_y, groups, 3, place_lanes))], axis=3
            )
            held_all = swapped(near.reshape(rows_y * groups, 3, -1), spread)
            held_all = held_all.reshape(pieces_count, box_cells + place_lanes)
            held_places = held_all[:, box_cells : box_cells + 2].astype(jnp.int32)
            held = held_all[:, :box_cells]
            rows_onehot = placement(held_places[:, 0], extent, grid_edge)
            cols_onehot = placement(held_places[:, 1], extent, grid_edge)
            rows_cut = rows_onehot.astype(jnp.bfloat16)
            cols_cut = cols_onehot.astype(jnp.bfloat16)
        else:
            held = swapped(near.reshape(rows_y * groups, 3, box_cells), spread)
        held = held.reshape(pieces_count, extent, extent)
        column_placed = jnp.einsum("kij,kgj->kig", held, cols_onehot, precision=matmul_precision)
        plane_sum = jnp.einsum(
            "khi,kig->hg", rows_onehot, column_placed, precision=matmul_precision
        ).reshape(grid_cells)
        density_plane = plane_sum + core_plane
        if sweep_index == STEPS - 1:
            gathered = swapped(jnp.broadcast_to(density_plane, (groups, grid_cells)), "group")
            rho_values = gathered[:slab_rows]
        potential = potential_of(external_plane, density_plane).reshape(grid_edge, grid_edge)
        row_windows = jnp.einsum(
            "khi,hg->kig", rows_cut, potential, preferred_element_type=jnp.float32
        ).astype(jnp.bfloat16)
        cut = jnp.einsum(
            "kig,kgj->kij", row_windows, cols_cut, preferred_element_type=jnp.float32
        ).astype(jnp.bfloat16)
        if sweep_index == STEPS - 1:
            cut, rho_values = lax.optimization_barrier((cut, rho_values))
        cut = swapped(cut.reshape(rows_y * groups, 3, box_cells), spread)
        cut = cut.reshape(rows_y, groups, 3, box_cells)[:, :slab_rows]
        cut = jnp.swapaxes(cut, 1, 2)
        back_parts = jnp.stack(
            [shifted(cut[:, 2], "rz", 1), cut[:, 1], shifted(cut[:, 0], "rz", -1)]
        ).reshape(3 * row_planes, box_cells)
        windows = lax.dynamic_slice_in_dim(back_parts, window_start, extent, 0).astype(jnp.float32)
        gradient = kinetic_part + separable(synthesis.T, windows[None] * orbital)
        current = current - step_size * gradient
    return (current, rho_values)


def solution(mesh):
    regions = mesh.shape["region"]
    rows_y = 4 if regions % 4 == 0 else 1
    torus = Mesh(
        mesh.devices.reshape(regions // rows_y, rows_y, mesh.shape["group"]), ("rz", "ry", "group")
    )
    every = ("rz", "ry", "group")
    return jax.shard_map(
        on_device,
        mesh=torus,
        in_specs=(
            P(every, None, None),
            P(None, every),
            P(every),
            P(("rz", "ry"), None),
            P(("rz", "ry"), None),
        ),
        out_specs=(P(every, None, None), P(("rz", "ry"), None)),
        check_vma=False,
    )
```

```python
import math

import jax
import numpy as np
import jax.numpy as jnp
from jax import lax
from jax.sharding import Mesh
from jax.sharding import PartitionSpec as P

STEPS = 2

step_size = 0.1
matmul_precision = lax.Precision.HIGH


def passed_along(value, axis, by):
    count = lax.axis_size(axis)
    return lax.ppermute(value, axis, [(i, (i + by) % count) for i in range(count)])


def filter_matrix(extent):
    offset_index = (np.arange(extent)[:, None] - np.arange(extent)[None, :] + 8).astype(np.float32)
    tap_grid = np.arange(16).astype(np.float32)
    tap_values = np.exp(-0.5 * ((tap_grid - 7.5) / 1.2) ** 2)
    norm_value = np.sqrt(np.sum(tap_values * tap_values))
    values = np.exp(-0.5 * ((offset_index - 7.5) / 1.2) ** 2) / norm_value
    inside = (offset_index >= 0.0) & (offset_index <= 15.0)
    return np.where(inside, values, 0.0).astype(np.float32)


def kinetic_matrix(extent):
    distance = np.arange(extent)[:, None] - np.arange(extent)[None, :]
    magnitude = np.abs(distance)
    parity = 1.0 - 2.0 * (magnitude % 2)
    spread = np.maximum(magnitude, 1).astype(np.float64)
    values = parity / (spread * spread)
    values = np.where(magnitude == 0, math.pi**2 / 6.0, values)
    return np.where(magnitude <= 14, values, 0.0).astype(np.float32)


def separable(matrix, box_values):
    members, extent, plane_cells = box_values.shape
    cube_values = box_values.reshape(members, extent, extent, extent)
    cube_values = jnp.einsum("ij,fjyx->fiyx", matrix, cube_values, precision=matmul_precision)
    cube_values = jnp.einsum("ij,fzjx->fzix", matrix, cube_values, precision=matmul_precision)
    cube_values = jnp.einsum("ij,fzyj->fzyi", matrix, cube_values, precision=matmul_precision)
    return cube_values.reshape(members, extent, plane_cells)


def kinetic_term(matrix, box_values):
    members, extent, plane_cells = box_values.shape
    cube_values = box_values.reshape(members, extent, extent, extent)
    along_planes = jnp.einsum("ij,fjyx->fiyx", matrix, cube_values, precision=matmul_precision)
    along_rows = jnp.einsum("ij,fzjx->fzix", matrix, cube_values, precision=matmul_precision)
    along_columns = jnp.einsum("ij,fzyj->fzyi", matrix, cube_values, precision=matmul_precision)
    return (along_planes + along_rows + along_columns).reshape(members, extent, plane_cells)


def potential_of(external, rho_values):
    return (external.astype(jnp.float32) - jnp.cbrt(3.0 / math.pi * rho_values)).astype(
        jnp.bfloat16
    )


def placement(starts, extent, edge):
    grid_index = jnp.arange(edge)[None, :, None]
    box_index = jnp.arange(extent)[None, None, :]
    target = jnp.mod(starts[:, None, None] + box_index, edge)
    return (grid_index == target).astype(jnp.float32)


def shifted(value, axis, by):
    count = lax.axis_size(axis)
    return lax.ppermute(value, axis, [(i, (i + by) % count) for i in range(count)])


def swapped(value, axis):
    return lax.all_to_all(value, axis, 0, 0, tiled=True)


def on_device(coefficients, box_offset, occupation, external_potential, core_density):
    members, extent, box_cells = coefficients.shape
    slab_rows, grid_cells = external_potential.shape
    rows_z, rows_y = lax.axis_size("rz"), lax.axis_size("ry")
    regions = rows_z * rows_y
    groups = lax.axis_size("group")
    grid_edge = math.isqrt(grid_cells)
    total_planes = slab_rows * regions
    reach_regions = extent // (2 * slab_rows)
    row_planes = rows_y * slab_rows
    coverage = float(total_planes * grid_cells) / float(members * regions * groups * extent**3)
    weight = coverage * occupation[0]
    synthesis = filter_matrix(extent)
    smoothing = (synthesis.astype(np.float64) @ synthesis.T.astype(np.float64)).astype(np.float32)
    kinetic_op = kinetic_matrix(extent)
    y_index = lax.axis_index("ry")
    region_index = lax.axis_index("rz") * rows_y + y_index
    base_plane = region_index * slab_rows - reach_regions * slab_rows
    plane_shift = jnp.mod(box_offset[0, 0] - base_plane, total_planes)
    window_start = plane_shift + slab_rows * y_index
    owned_plane = jnp.minimum(lax.axis_index("group"), slab_rows - 1)
    core_plane = lax.dynamic_index_in_dim(core_density, owned_plane, 0, keepdims=False)
    external_plane = lax.dynamic_index_in_dim(external_potential, owned_plane, 0, keepdims=False)
    place_lanes = 128
    places = jnp.stack([box_offset[1, 0], box_offset[2, 0]]).astype(jnp.float32)
    places = jnp.pad(places, (0, place_lanes - 2))
    spread = ("ry", "group")
    pieces_count = 3 * rows_y * groups
    idle = groups - slab_rows
    current = coefficients
    rho_values = None
    orbital = separable(synthesis, current)
    for sweep_index in range(STEPS):
        kinetic_part = kinetic_term(kinetic_op, current)
        weighted = weight * orbital[0] * orbital[0]
        window = jnp.zeros((3 * row_planes, box_cells), jnp.float32)
        window = lax.dynamic_update_slice_in_dim(window, weighted, window_start, 0)
        parts = window.reshape(3, rows_y, slab_rows, box_cells)
        if sweep_index == 0:
            piece_cells = slab_rows * box_cells
            tagged = jnp.concatenate(
                [
                    parts[::2].reshape(2, rows_y, piece_cells),
                    jnp.broadcast_to(places, (2, rows_y, place_lanes)),
                ],
                axis=2,
            )
            got_below = shifted(tagged[1], "rz", 1)
            got_above = shifted(tagged[0], "rz", -1)
            from_below = got_below[:, :piece_cells].reshape(rows_y, slab_rows, box_cells)
            from_above = got_above[:, :piece_cells].reshape(rows_y, slab_rows, box_cells)
            near_places = jnp.stack([got_below[0, piece_cells:], places, got_above[0, piece_cells:]])
        else:
            from_below = shifted(parts[2], "rz", 1)
            from_above = shifted(parts[0], "rz", -1)
        near = jnp.stack([from_below, parts[1], from_above], axis=2)
        near = jnp.pad(near, ((0, 0), (0, idle), (0, 0), (0, 0)))
        if sweep_index == 0:
            near = jnp.concatenate(
                [near, jnp.broadcast_to(near_places, (rows_y, groups, 3, place_lanes))], axis=3
            )
            held_all = swapped(near.reshape(rows_y * groups, 3, -1), spread)
            held_all = held_all.reshape(pieces_count, box_cells + place_lanes)
            held_places = held_all[:, box_cells : box_cells + 2].astype(jnp.int32)
            held = held_all[:, :box_cells]
            rows_onehot = placement(held_places[:, 0], extent, grid_edge)
            cols_onehot = placement(held_places[:, 1], extent, grid_edge)
            rows_cut = rows_onehot.astype(jnp.bfloat16)
            cols_cut = cols_onehot.astype(jnp.bfloat16)
        else:
            held = swapped(near.reshape(rows_y * groups, 3, box_cells), spread)
        held = held.reshape(pieces_count, extent, extent)
        column_placed = jnp.einsum("kij,kgj->kig", held, cols_onehot, precision=matmul_precision)
        plane_sum = jnp.einsum(
            "khi,kig->hg", rows_onehot, column_placed, precision=matmul_precision
        ).reshape(grid_cells)
        density_plane = plane_sum + core_plane
        if sweep_index == STEPS - 1:
            gathered = swapped(jnp.broadcast_to(density_plane, (groups, grid_cells)), "group")
            rho_values = gathered[:slab_rows]
        potential = potential_of(external_plane, density_plane).reshape(grid_edge, grid_edge)
        row_windows = jnp.einsum(
            "khi,hg->kig", rows_cut, potential, preferred_element_type=jnp.float32
        ).astype(jnp.bfloat16)
        cut = jnp.einsum(
            "kig,kgj->kij", row_windows, cols_cut, preferred_element_type=jnp.float32
        ).astype(jnp.bfloat16)
        cut = swapped(cut.reshape(rows_y * groups, 3, box_cells), spread)
        cut = cut.reshape(rows_y, groups, 3, box_cells)[:, :slab_rows]
        cut = jnp.swapaxes(cut, 1, 2)
        back_parts = jnp.stack(
            [shifted(cut[:, 2], "rz", 1), cut[:, 1], shifted(cut[:, 0], "rz", -1)]
        ).reshape(3 * row_planes, box_cells)
        windows = lax.dynamic_slice_in_dim(back_parts, window_start, extent, 0).astype(jnp.float32)
        product = windows[None] * orbital
        gradient = kinetic_part + separable(synthesis.T, product)
        current = current - step_size * gradient
        if sweep_index < STEPS - 1:
            orbital = orbital - step_size * (
                separable(synthesis, kinetic_part) + separable(smoothing, product)
            )
    return (current, rho_values)


def solution(mesh):
    regions = mesh.shape["region"]
    rows_y = 4 if regions % 4 == 0 else 1
    torus = Mesh(
        mesh.devices.reshape(regions // rows_y, rows_y, mesh.shape["group"]), ("rz", "ry", "group")
    )
    every = ("rz", "ry", "group")
    return jax.shard_map(
        on_device,
        mesh=torus,
        in_specs=(
            P(every, None, None),
            P(None, every),
            P(every),
            P(("rz", "ry"), None),
            P(("rz", "ry"), None),
        ),
        out_specs=(P(every, None, None), P(("rz", "ry"), None)),
        check_vma=False,
    )
```

```python
import math

import jax
import numpy as np
import jax.numpy as jnp
from jax import lax
from jax.sharding import Mesh
from jax.sharding import PartitionSpec as P

STEPS = 2

step_size = 0.1
matmul_precision = lax.Precision.HIGH


def passed_along(value, axis, by):
    count = lax.axis_size(axis)
    return lax.ppermute(value, axis, [(i, (i + by) % count) for i in range(count)])


def filter_matrix(extent):
    offset_index = (np.arange(extent)[:, None] - np.arange(extent)[None, :] + 8).astype(np.float32)
    tap_grid = np.arange(16).astype(np.float32)
    tap_values = np.exp(-0.5 * ((tap_grid - 7.5) / 1.2) ** 2)
    norm_value = np.sqrt(np.sum(tap_values * tap_values))
    values = np.exp(-0.5 * ((offset_index - 7.5) / 1.2) ** 2) / norm_value
    inside = (offset_index >= 0.0) & (offset_index <= 15.0)
    return np.where(inside, values, 0.0).astype(np.float32)


def kinetic_matrix(extent):
    distance = np.arange(extent)[:, None] - np.arange(extent)[None, :]
    magnitude = np.abs(distance)
    parity = 1.0 - 2.0 * (magnitude % 2)
    spread = np.maximum(magnitude, 1).astype(np.float64)
    values = parity / (spread * spread)
    values = np.where(magnitude == 0, math.pi**2 / 6.0, values)
    return np.where(magnitude <= 14, values, 0.0).astype(np.float32)


def separable(matrix, box_values):
    members, extent, plane_cells = box_values.shape
    cube_values = box_values.reshape(members, extent, extent, extent)
    cube_values = jnp.einsum("ij,fjyx->fiyx", matrix, cube_values, precision=matmul_precision)
    cube_values = jnp.einsum("ij,fzjx->fzix", matrix, cube_values, precision=matmul_precision)
    cube_values = jnp.einsum("ij,fzyj->fzyi", matrix, cube_values, precision=matmul_precision)
    return cube_values.reshape(members, extent, plane_cells)


def kinetic_term(matrix, box_values):
    members, extent, plane_cells = box_values.shape
    cube_values = box_values.reshape(members, extent, extent, extent)
    along_planes = jnp.einsum("ij,fjyx->fiyx", matrix, cube_values, precision=matmul_precision)
    along_rows = jnp.einsum("ij,fzjx->fzix", matrix, cube_values, precision=matmul_precision)
    along_columns = jnp.einsum("ij,fzyj->fzyi", matrix, cube_values, precision=matmul_precision)
    return (along_planes + along_rows + along_columns).reshape(members, extent, plane_cells)


def potential_of(external, rho_values):
    return (external.astype(jnp.float32) - jnp.cbrt(3.0 / math.pi * rho_values)).astype(
        jnp.bfloat16
    )


def placement(starts, extent, edge):
    grid_index = jnp.arange(edge)[None, :, None]
    box_index = jnp.arange(extent)[None, None, :]
    target = jnp.mod(starts[:, None, None] + box_index, edge)
    return (grid_index == target).astype(jnp.float32)


def shifted(value, axis, by):
    count = lax.axis_size(axis)
    return lax.ppermute(value, axis, [(i, (i + by) % count) for i in range(count)])


def swapped(value, axis):
    return lax.all_to_all(value, axis, 0, 0, tiled=True)


def on_device(coefficients, box_offset, occupation, external_potential, core_density):
    members, extent, box_cells = coefficients.shape
    slab_rows, grid_cells = external_potential.shape
    rows_z, rows_y = lax.axis_size("rz"), lax.axis_size("ry")
    regions = rows_z * rows_y
    groups = lax.axis_size("group")
    grid_edge = math.isqrt(grid_cells)
    total_planes = slab_rows * regions
    reach_regions = extent // (2 * slab_rows)
    row_planes = rows_y * slab_rows
    coverage = float(total_planes * grid_cells) / float(members * regions * groups * extent**3)
    weight = coverage * occupation[0]
    synthesis = filter_matrix(extent)
    kinetic_op = kinetic_matrix(extent)
    y_index = lax.axis_index("ry")
    region_index = lax.axis_index("rz") * rows_y + y_index
    base_plane = region_index * slab_rows - reach_regions * slab_rows
    plane_shift = jnp.mod(box_offset[0, 0] - base_plane, total_planes)
    window_start = plane_shift + slab_rows * y_index
    owned_plane = jnp.minimum(lax.axis_index("group"), slab_rows - 1)
    core_plane = lax.dynamic_index_in_dim(core_density, owned_plane, 0, keepdims=False)
    external_plane = lax.dynamic_index_in_dim(external_potential, owned_plane, 0, keepdims=False)
    place_lanes = 128
    places = jnp.stack([box_offset[1, 0], box_offset[2, 0]]).astype(jnp.float32)
    places = jnp.pad(places, (0, place_lanes - 2))
    spread = ("ry", "group")
    pieces_count = 3 * rows_y * groups
    idle = groups - slab_rows
    current = coefficients
    rho_values = None
    for sweep_index in range(STEPS):
        orbital = separable(synthesis, current)
        kinetic_part = kinetic_term(kinetic_op, current)
        weighted = weight * orbital[0] * orbital[0]
        window = jnp.zeros((3 * row_planes, box_cells), jnp.float32)
        window = lax.dynamic_update_slice_in_dim(window, weighted, window_start, 0)
        parts = window.reshape(3, rows_y, slab_rows, box_cells)
        outgoing = jnp.pad(
            jnp.transpose(parts, (1, 2, 0, 3)), ((0, 0), (0, idle), (0, 0), (0, 0))
        )
        if sweep_index == 0:
            outgoing = jnp.concatenate(
                [outgoing, jnp.broadcast_to(places, (rows_y, groups, 3, place_lanes))], axis=3
            )
        lanes = outgoing.shape[-1]
        arrived = swapped(outgoing.reshape(rows_y * groups, 3, lanes), spread)
        from_below = shifted(arrived[:, 2], "rz", 1)
        from_above = shifted(arrived[:, 0], "rz", -1)
        held = jnp.stack([from_below, arrived[:, 1], from_above], axis=1).reshape(
            pieces_count, lanes
        )
        if sweep_index == 0:
            held_places = held[:, box_cells : box_cells + 2].astype(jnp.int32)
            held = held[:, :box_cells]
            rows_onehot = placement(held_places[:, 0], extent, grid_edge)
            cols_onehot = placement(held_places[:, 1], extent, grid_edge)
            rows_cut = rows_onehot.astype(jnp.bfloat16)
            cols_cut = cols_onehot.astype(jnp.bfloat16)
        held = held.reshape(pieces_count, extent, extent)
        column_placed = jnp.einsum("kij,kgj->kig", held, cols_onehot, precision=matmul_precision)
        plane_sum = jnp.einsum(
            "khi,kig->hg", rows_onehot, column_placed, precision=matmul_precision
        ).reshape(grid_cells)
        density_plane = plane_sum + core_plane
        if sweep_index == STEPS - 1:
            gathered = swapped(jnp.broadcast_to(density_plane, (groups, grid_cells)), "group")
            rho_values = gathered[:slab_rows]
        potential = potential_of(external_plane, density_plane).reshape(grid_edge, grid_edge)
        row_windows = jnp.einsum(
            "khi,hg->kig", rows_cut, potential, preferred_element_type=jnp.float32
        ).astype(jnp.bfloat16)
        cut = jnp.einsum(
            "kig,kgj->kij", row_windows, cols_cut, preferred_element_type=jnp.float32
        ).astype(jnp.bfloat16)
        cut = cut.reshape(rows_y * groups, 3, box_cells)
        returned = jnp.stack(
            [shifted(cut[:, 2], "rz", 1), cut[:, 1], shifted(cut[:, 0], "rz", -1)], axis=1
        )
        returned = swapped(returned, spread).reshape(rows_y, groups, 3, box_cells)[:, :slab_rows]
        back_parts = jnp.transpose(returned, (2, 0, 1, 3)).reshape(3 * row_planes, box_cells)
        windows = lax.dynamic_slice_in_dim(back_parts, window_start, extent, 0).astype(jnp.float32)
        gradient = kinetic_part + separable(synthesis.T, windows[None] * orbital)
        current = current - step_size * gradient
    return (current, rho_values)


def solution(mesh):
    regions = mesh.shape["region"]
    rows_y = 4 if regions % 4 == 0 else 1
    torus = Mesh(
        mesh.devices.reshape(regions // rows_y, rows_y, mesh.shape["group"]), ("rz", "ry", "group")
    )
    every = ("rz", "ry", "group")
    return jax.shard_map(
        on_device,
        mesh=torus,
        in_specs=(
            P(every, None, None),
            P(None, every),
            P(every),
            P(("rz", "ry"), None),
            P(("rz", "ry"), None),
        ),
        out_specs=(P(every, None, None), P(("rz", "ry"), None)),
        check_vma=False,
    )
```

```python
import math

import jax
import numpy as np
import jax.numpy as jnp
from jax import lax
from jax.sharding import Mesh
from jax.sharding import PartitionSpec as P

STEPS = 2

step_size = 0.1
matmul_precision = lax.Precision.HIGH


def passed_along(value, axis, by):
    count = lax.axis_size(axis)
    return lax.ppermute(value, axis, [(i, (i + by) % count) for i in range(count)])


def filter_matrix(extent):
    offset_index = (np.arange(extent)[:, None] - np.arange(extent)[None, :] + 8).astype(np.float32)
    tap_grid = np.arange(16).astype(np.float32)
    tap_values = np.exp(-0.5 * ((tap_grid - 7.5) / 1.2) ** 2)
    norm_value = np.sqrt(np.sum(tap_values * tap_values))
    values = np.exp(-0.5 * ((offset_index - 7.5) / 1.2) ** 2) / norm_value
    inside = (offset_index >= 0.0) & (offset_index <= 15.0)
    return np.where(inside, values, 0.0).astype(np.float32)


def kinetic_matrix(extent):
    distance = np.arange(extent)[:, None] - np.arange(extent)[None, :]
    magnitude = np.abs(distance)
    parity = 1.0 - 2.0 * (magnitude % 2)
    spread = np.maximum(magnitude, 1).astype(np.float64)
    values = parity / (spread * spread)
    values = np.where(magnitude == 0, math.pi**2 / 6.0, values)
    return np.where(magnitude <= 14, values, 0.0).astype(np.float32)


def separable(matrix, box_values):
    members, extent, plane_cells = box_values.shape
    cube_values = box_values.reshape(members, extent, extent, extent)
    cube_values = jnp.einsum("ij,fjyx->fiyx", matrix, cube_values, precision=matmul_precision)
    cube_values = jnp.einsum("ij,fzjx->fzix", matrix, cube_values, precision=matmul_precision)
    cube_values = jnp.einsum("ij,fzyj->fzyi", matrix, cube_values, precision=matmul_precision)
    return cube_values.reshape(members, extent, plane_cells)


def kinetic_term(matrix, box_values):
    members, extent, plane_cells = box_values.shape
    cube_values = box_values.reshape(members, extent, extent, extent)
    along_planes = jnp.einsum("ij,fjyx->fiyx", matrix, cube_values, precision=matmul_precision)
    along_rows = jnp.einsum("ij,fzjx->fzix", matrix, cube_values, precision=matmul_precision)
    along_columns = jnp.einsum("ij,fzyj->fzyi", matrix, cube_values, precision=matmul_precision)
    return (along_planes + along_rows + along_columns).reshape(members, extent, plane_cells)


def potential_of(external, rho_values):
    return (external.astype(jnp.float32) - jnp.cbrt(3.0 / math.pi * rho_values)).astype(
        jnp.bfloat16
    )


def placement(starts, extent, edge):
    grid_index = jnp.arange(edge)[None, :, None]
    box_index = jnp.arange(extent)[None, None, :]
    target = jnp.mod(starts[:, None, None] + box_index, edge)
    return (grid_index == target).astype(jnp.float32)


def shifted(value, axis, by):
    count = lax.axis_size(axis)
    return lax.ppermute(value, axis, [(i, (i + by) % count) for i in range(count)])


def swapped(value, axis):
    return lax.all_to_all(value, axis, 0, 0, tiled=True)


def on_device(coefficients, box_offset, occupation, external_potential, core_density):
    members, extent, box_cells = coefficients.shape
    slab_rows, grid_cells = external_potential.shape
    rows_z, rows_y = lax.axis_size("rz"), lax.axis_size("ry")
    regions = rows_z * rows_y
    groups = lax.axis_size("group")
    grid_edge = math.isqrt(grid_cells)
    total_planes = slab_rows * regions
    reach_regions = extent // (2 * slab_rows)
    row_planes = rows_y * slab_rows
    coverage = float(total_planes * grid_cells) / float(members * regions * groups * extent**3)
    weight = coverage * occupation[0]
    synthesis = filter_matrix(extent)
    kinetic_op = kinetic_matrix(extent)
    y_index = lax.axis_index("ry")
    region_index = lax.axis_index("rz") * rows_y + y_index
    base_plane = region_index * slab_rows - reach_regions * slab_rows
    plane_shift = jnp.mod(box_offset[0, 0] - base_plane, total_planes)
    window_start = plane_shift + slab_rows * y_index
    owned_plane = jnp.minimum(lax.axis_index("group"), slab_rows - 1)
    core_plane = lax.dynamic_index_in_dim(core_density, owned_plane, 0, keepdims=False)
    external_plane = lax.dynamic_index_in_dim(external_potential, owned_plane, 0, keepdims=False)
    place_lanes = 128
    places = jnp.stack([box_offset[1, 0], box_offset[2, 0]]).astype(jnp.float32)
    places = jnp.pad(places, (0, place_lanes - 2))
    spread = ("ry", "group")
    pieces_count = 3 * rows_y * groups
    idle = groups - slab_rows
    def sweep(sweep_index, state):
        current, rho_values = state
        orbital = separable(synthesis, current)
        kinetic_part = kinetic_term(kinetic_op, current)
        weighted = weight * orbital[0] * orbital[0]
        window = jnp.zeros((3 * row_planes, box_cells), jnp.float32)
        window = lax.dynamic_update_slice_in_dim(window, weighted, window_start, 0)
        parts = window.reshape(3, rows_y, slab_rows, box_cells)
        piece_cells = slab_rows * box_cells
        tagged = jnp.concatenate(
            [
                parts[::2].reshape(2, rows_y, piece_cells),
                jnp.broadcast_to(places, (2, rows_y, place_lanes)),
            ],
            axis=2,
        )
        got_below = shifted(tagged[1], "rz", 1)
        got_above = shifted(tagged[0], "rz", -1)
        from_below = got_below[:, :piece_cells].reshape(rows_y, slab_rows, box_cells)
        from_above = got_above[:, :piece_cells].reshape(rows_y, slab_rows, box_cells)
        near_places = jnp.stack([got_below[0, piece_cells:], places, got_above[0, piece_cells:]])
        near = jnp.stack([from_below, parts[1], from_above], axis=2)
        near = jnp.pad(near, ((0, 0), (0, idle), (0, 0), (0, 0)))
        near = jnp.concatenate(
            [near, jnp.broadcast_to(near_places, (rows_y, groups, 3, place_lanes))], axis=3
        )
        held_all = swapped(near.reshape(rows_y * groups, 3, -1), spread)
        held_all = held_all.reshape(pieces_count, box_cells + place_lanes)
        held_places = held_all[:, box_cells : box_cells + 2].astype(jnp.int32)
        held = held_all[:, :box_cells]
        rows_onehot = placement(held_places[:, 0], extent, grid_edge)
        cols_onehot = placement(held_places[:, 1], extent, grid_edge)
        rows_cut = rows_onehot.astype(jnp.bfloat16)
        cols_cut = cols_onehot.astype(jnp.bfloat16)
        held = held.reshape(pieces_count, extent, extent)
        column_placed = jnp.einsum("kij,kgj->kig", held, cols_onehot, precision=matmul_precision)
        plane_sum = jnp.einsum(
            "khi,kig->hg", rows_onehot, column_placed, precision=matmul_precision
        ).reshape(grid_cells)
        density_plane = plane_sum + core_plane
        rho_values = lax.cond(
            sweep_index == STEPS - 1,
            lambda plane: swapped(jnp.broadcast_to(plane, (groups, grid_cells)), "group")[:slab_rows],
            lambda plane: rho_values,
            density_plane,
        )
        potential = potential_of(external_plane, density_plane).reshape(grid_edge, grid_edge)
        row_windows = jnp.einsum(
            "khi,hg->kig", rows_cut, potential, preferred_element_type=jnp.float32
        ).astype(jnp.bfloat16)
        cut = jnp.einsum(
            "kig,kgj->kij", row_windows, cols_cut, preferred_element_type=jnp.float32
        ).astype(jnp.bfloat16)
        cut = swapped(cut.reshape(rows_y * groups, 3, box_cells), spread)
        cut = cut.reshape(rows_y, groups, 3, box_cells)[:, :slab_rows]
        cut = jnp.swapaxes(cut, 1, 2)
        back_parts = jnp.stack(
            [shifted(cut[:, 2], "rz", 1), cut[:, 1], shifted(cut[:, 0], "rz", -1)]
        ).reshape(3 * row_planes, box_cells)
        windows = lax.dynamic_slice_in_dim(back_parts, window_start, extent, 0).astype(jnp.float32)
        gradient = kinetic_part + separable(synthesis.T, windows[None] * orbital)
        current = current - step_size * gradient
        return (current, rho_values)

    empty = jnp.zeros((slab_rows, grid_cells), jnp.float32)
    current, rho_values = lax.fori_loop(0, STEPS, sweep, (coefficients, empty))
    return (current, rho_values)


def solution(mesh):
    regions = mesh.shape["region"]
    rows_y = 4 if regions % 4 == 0 else 1
    torus = Mesh(
        mesh.devices.reshape(regions // rows_y, rows_y, mesh.shape["group"]), ("rz", "ry", "group")
    )
    every = ("rz", "ry", "group")
    return jax.shard_map(
        on_device,
        mesh=torus,
        in_specs=(
            P(every, None, None),
            P(None, every),
            P(every),
            P(("rz", "ry"), None),
            P(("rz", "ry"), None),
        ),
        out_specs=(P(every, None, None), P(("rz", "ry"), None)),
        check_vma=False,
    )
```

```python
import math

import jax
import numpy as np
import jax.numpy as jnp
from jax import lax
from jax.sharding import Mesh
from jax.sharding import PartitionSpec as P

STEPS = 2

step_size = 0.1
matmul_precision = lax.Precision.HIGH


def passed_along(value, axis, by):
    count = lax.axis_size(axis)
    return lax.ppermute(value, axis, [(i, (i + by) % count) for i in range(count)])


def filter_matrix(extent):
    offset_index = (np.arange(extent)[:, None] - np.arange(extent)[None, :] + 8).astype(np.float32)
    tap_grid = np.arange(16).astype(np.float32)
    tap_values = np.exp(-0.5 * ((tap_grid - 7.5) / 1.2) ** 2)
    norm_value = np.sqrt(np.sum(tap_values * tap_values))
    values = np.exp(-0.5 * ((offset_index - 7.5) / 1.2) ** 2) / norm_value
    inside = (offset_index >= 0.0) & (offset_index <= 15.0)
    return np.where(inside, values, 0.0).astype(np.float32)


def kinetic_matrix(extent):
    distance = np.arange(extent)[:, None] - np.arange(extent)[None, :]
    magnitude = np.abs(distance)
    parity = 1.0 - 2.0 * (magnitude % 2)
    spread = np.maximum(magnitude, 1).astype(np.float64)
    values = parity / (spread * spread)
    values = np.where(magnitude == 0, math.pi**2 / 6.0, values)
    return np.where(magnitude <= 14, values, 0.0).astype(np.float32)


def separable(matrix, box_values):
    members, extent, plane_cells = box_values.shape
    cube_values = box_values.reshape(members, extent, extent, extent)
    cube_values = jnp.einsum("ij,fjyx->fiyx", matrix, cube_values, precision=matmul_precision)
    cube_values = jnp.einsum("ij,fzjx->fzix", matrix, cube_values, precision=matmul_precision)
    cube_values = jnp.einsum("ij,fzyj->fzyi", matrix, cube_values, precision=matmul_precision)
    return cube_values.reshape(members, extent, plane_cells)


def kinetic_term(matrix, box_values):
    members, extent, plane_cells = box_values.shape
    cube_values = box_values.reshape(members, extent, extent, extent)
    along_planes = jnp.einsum("ij,fjyx->fiyx", matrix, cube_values, precision=matmul_precision)
    along_rows = jnp.einsum("ij,fzjx->fzix", matrix, cube_values, precision=matmul_precision)
    along_columns = jnp.einsum("ij,fzyj->fzyi", matrix, cube_values, precision=matmul_precision)
    return (along_planes + along_rows + along_columns).reshape(members, extent, plane_cells)


def potential_of(external, rho_values):
    return (external.astype(jnp.float32) - jnp.cbrt(3.0 / math.pi * rho_values)).astype(
        jnp.bfloat16
    )


def placement(starts, extent, edge):
    grid_index = jnp.arange(edge)[None, :, None]
    box_index = jnp.arange(extent)[None, None, :]
    target = jnp.mod(starts[:, None, None] + box_index, edge)
    return (grid_index == target).astype(jnp.float32)


def shifted(value, axis, by):
    count = lax.axis_size(axis)
    return lax.ppermute(value, axis, [(i, (i + by) % count) for i in range(count)])


def swapped(value, axis):
    return lax.all_to_all(value, axis, 0, 0, tiled=True)


def on_device(coefficients, box_offset, occupation, external_potential, core_density):
    members, extent, box_cells = coefficients.shape
    slab_rows, grid_cells = external_potential.shape
    rows_z, rows_y = lax.axis_size("rz"), lax.axis_size("ry")
    regions = rows_z * rows_y
    groups = lax.axis_size("group")
    grid_edge = math.isqrt(grid_cells)
    total_planes = slab_rows * regions
    reach_regions = extent // (2 * slab_rows)
    row_planes = rows_y * slab_rows
    coverage = float(total_planes * grid_cells) / float(members * regions * groups * extent**3)
    weight = coverage * occupation[0]
    synthesis = filter_matrix(extent)
    kinetic_op = kinetic_matrix(extent)
    y_index = lax.axis_index("ry")
    region_index = lax.axis_index("rz") * rows_y + y_index
    base_plane = region_index * slab_rows - reach_regions * slab_rows
    plane_shift = jnp.mod(box_offset[0, 0] - base_plane, total_planes)
    window_start = plane_shift + slab_rows * y_index
    owners = [p if p < slab_rows - 1 else groups - 2 for p in range(slab_rows)]
    plane_of_member = [owners.index(g) if g in owners else 0 for g in range(groups)]
    owned_plane = jnp.asarray(plane_of_member, jnp.int32)[lax.axis_index("group")]
    core_plane = lax.dynamic_index_in_dim(core_density, owned_plane, 0, keepdims=False)
    external_plane = lax.dynamic_index_in_dim(external_potential, owned_plane, 0, keepdims=False)
    place_lanes = 128
    places = jnp.stack([box_offset[1, 0], box_offset[2, 0]]).astype(jnp.float32)
    places = jnp.pad(places, (0, place_lanes - 2))
    spread = ("ry", "group")
    pieces_count = 3 * rows_y * groups
    current = coefficients
    rho_values = None
    for sweep_index in range(STEPS):
        orbital = separable(synthesis, current)
        kinetic_part = kinetic_term(kinetic_op, current)
        weighted = weight * orbital[0] * orbital[0]
        window = jnp.zeros((3 * row_planes, box_cells), jnp.float32)
        window = lax.dynamic_update_slice_in_dim(window, weighted, window_start, 0)
        parts = window.reshape(3, rows_y, slab_rows, box_cells)
        if sweep_index == 0:
            piece_cells = slab_rows * box_cells
            tagged = jnp.concatenate(
                [
                    parts[::2].reshape(2, rows_y, piece_cells),
                    jnp.broadcast_to(places, (2, rows_y, place_lanes)),
                ],
                axis=2,
            )
            got_below = shifted(tagged[1], "rz", 1)
            got_above = shifted(tagged[0], "rz", -1)
            from_below = got_below[:, :piece_cells].reshape(rows_y, slab_rows, box_cells)
            from_above = got_above[:, :piece_cells].reshape(rows_y, slab_rows, box_cells)
            near_places = jnp.stack([got_below[0, piece_cells:], places, got_above[0, piece_cells:]])
        else:
            from_below = shifted(parts[2], "rz", 1)
            from_above = shifted(parts[0], "rz", -1)
        near = jnp.stack([from_below, parts[1], from_above], axis=2)
        near = near[:, np.asarray(plane_of_member)]
        if sweep_index == 0:
            near = jnp.concatenate(
                [near, jnp.broadcast_to(near_places, (rows_y, groups, 3, place_lanes))], axis=3
            )
            held_all = swapped(near.reshape(rows_y * groups, 3, -1), spread)
            held_all = held_all.reshape(pieces_count, box_cells + place_lanes)
            held_places = held_all[:, box_cells : box_cells + 2].astype(jnp.int32)
            held = held_all[:, :box_cells]
            rows_onehot = placement(held_places[:, 0], extent, grid_edge)
            cols_onehot = placement(held_places[:, 1], extent, grid_edge)
            rows_cut = rows_onehot.astype(jnp.bfloat16)
            cols_cut = cols_onehot.astype(jnp.bfloat16)
        else:
            held = swapped(near.reshape(rows_y * groups, 3, box_cells), spread)
        held = held.reshape(pieces_count, extent, extent)
        column_placed = jnp.einsum("kij,kgj->kig", held, cols_onehot, precision=matmul_precision)
        plane_sum = jnp.einsum(
            "khi,kig->hg", rows_onehot, column_placed, precision=matmul_precision
        ).reshape(grid_cells)
        density_plane = plane_sum + core_plane
        if sweep_index == STEPS - 1:
            gathered = swapped(jnp.broadcast_to(density_plane, (groups, grid_cells)), "group")
            rho_values = gathered[np.asarray(owners)]
        potential = potential_of(external_plane, density_plane).reshape(grid_edge, grid_edge)
        row_windows = jnp.einsum(
            "khi,hg->kig", rows_cut, potential, preferred_element_type=jnp.float32
        ).astype(jnp.bfloat16)
        cut = jnp.einsum(
            "kig,kgj->kij", row_windows, cols_cut, preferred_element_type=jnp.float32
        ).astype(jnp.bfloat16)
        cut = swapped(cut.reshape(rows_y * groups, 3, box_cells), spread)
        cut = cut.reshape(rows_y, groups, 3, box_cells)[:, np.asarray(owners)]
        cut = jnp.swapaxes(cut, 1, 2)
        back_parts = jnp.stack(
            [shifted(cut[:, 2], "rz", 1), cut[:, 1], shifted(cut[:, 0], "rz", -1)]
        ).reshape(3 * row_planes, box_cells)
        windows = lax.dynamic_slice_in_dim(back_parts, window_start, extent, 0).astype(jnp.float32)
        gradient = kinetic_part + separable(synthesis.T, windows[None] * orbital)
        current = current - step_size * gradient
    return (current, rho_values)


def solution(mesh):
    regions = mesh.shape["region"]
    rows_y = 4 if regions % 4 == 0 else 1
    torus = Mesh(
        mesh.devices.reshape(regions // rows_y, rows_y, mesh.shape["group"]), ("rz", "ry", "group")
    )
    every = ("rz", "ry", "group")
    return jax.shard_map(
        on_device,
        mesh=torus,
        in_specs=(
            P(every, None, None),
            P(None, every),
            P(every),
            P(("rz", "ry"), None),
            P(("rz", "ry"), None),
        ),
        out_specs=(P(every, None, None), P(("rz", "ry"), None)),
        check_vma=False,
    )
```
